32 devices in a mesh: groups: 2 (over y), tensor: 4 (over z), seq: 2 (over x), load: 2 (over core).
Axes of the slice: x: 2, y: 2, z: 4, core: 2. Of those that a mesh axis runs over, the one named last changes fastest.
Arguments:
- tokens: bfloat16 [1024, 16384], P(('groups', 'tensor'), ('seq', 'load')), parts along dimension 0, may hold values from -21 to 21
- weight_query: bfloat16 [16384, 16384], P(('seq', 'load'), 'tensor'), may hold values from -0.046875 to 0.046875
- weight_keyval: bfloat16 [16384, 2048], P(('seq', 'load'), 'tensor'), may hold values from -0.046875 to 0.046875
- down_query: bfloat16 [16384, 1024], P(('seq', 'load'), ('groups', 'tensor')), parts along dimension 1, may hold values from -0.046875 to 0.046875
- down_keyval: bfloat16 [16384, 1024], P(('seq', 'load'), ('groups', 'tensor')), parts along dimension 1, may hold values from -0.046875 to 0.046875
- up_query: bfloat16 [1024, 16384], P(('groups', 'load'), 'tensor'), parts along dimension 0, may hold values from -0.5 to 0.5
- up_keyval: bfloat16 [1024, 2048], P(('groups', 'load'), 'tensor'), parts along dimension 0, may hold values from -0.5 to 0.5
- adapter_rank: int32 [8], P('groups'), parts along dimension 0, may hold values from 8 to 128, as said below
- token_lengths: int32 [8], P('groups'), parts along dimension 0, may hold values from 1 to 384, 512 in all
- adapter_slot: int32 [8], P('groups'), parts along dimension 0, may hold values from 0 to 3, each once
Outputs:
- context: bfloat16 [1024, 16384], P(('groups', 'seq', 'load'), 'tensor'), parts along dimension 0
- kv_cache: bfloat16 [1024, 2048], P(('groups', 'seq', 'load'), 'tensor'), parts along dimension 0
The draws below stay inside these ranges and needn't reach their ends.
There are 2 independent parts, one for each index of `groups`. The reference program is written for one: setup_inputs(seed, part) draws one part's arguments, and reference() takes and returns one part's arrays. A program takes and returns all parts, laid end to end along the dimension named above; an argument that names none is the same for every part. Nothing has to cross between parts.
Inputs may be any that keep to these rules, and one draw needn't show every extreme that they name: `adapter_rank`: each rank is a power of two; some tenant has rank 128 and some has rank 8. `token_lengths`: the lengths sum to 512; some tenant has exactly 384 tokens. `adapter_slot`: each slot belongs to exactly one tenant.
All inputs are finite; a program needn't handle non-finite values.
Results may differ from the reference program's by a relative error of at most 0.0025.
The reference program's roundings to bfloat16 on the way count: a program that leaves them out, or rounds other values in their place, can miss the bound.
Values may be sent and summed in bfloat16 or wider, within the bound.
No kernel may reach another device: no remote copies, remote signals or barrier semaphores. Data moves between devices by JAX's collectives and lax.ppermute only.
A program may use at most 128 MiB of HBM per device.

```python
import math
import jax
import jax.numpy as jnp
import numpy as np
from jax import lax

D = 16384
HEADS = 128
KV_HEADS = 8
HEAD_DIM = 128
RMAX = 128
TENANTS = 4
TOKENS = 512
MOST = 384


def draw_tokens(key, part):
    normal_draw = jnp.clip(jax.random.normal(key, (TOKENS, D), jnp.float32), -6.0, 6.0)
    return normal_draw.astype(jnp.bfloat16)


def draw_adapter_rank(key, part):
    part_key = jax.random.fold_in(jax.random.fold_in(key, 29), part)
    level_count = RMAX.bit_length() - 3
    levels = jax.random.randint(jax.random.fold_in(part_key, 21), (TENANTS,), 0, level_count)
    rank_values = jnp.left_shift(jnp.full((TENANTS,), 8, jnp.int32), levels.astype(jnp.int32))
    top_index = jax.random.randint(jax.random.fold_in(part_key, 22), (), 0, TENANTS)
    low_index = (top_index + 1 + jax.random.randint(jax.random.fold_in(part_key, 23), (), 0, TENANTS - 1)) % TENANTS
    rank_values = rank_values.at[top_index].set(RMAX)
    rank_values = rank_values.at[low_index].set(8)
    return rank_values.astype(jnp.int32)


def block_levels(rng, shape, shards, least, largest):
    level = 1.0
    for dim, blocks in shards:
        draws = jax.random.uniform(jax.random.fold_in(jax.random.fold_in(rng, 6), dim), (blocks,), jnp.float32, least / len(shards), largest / len(shards))
        level = level * jnp.repeat(jnp.exp(draws), shape[dim] // blocks).reshape((-1,) + (1,) * (len(shape) - 1 - dim))
    return level


def profile(count, total, limit, slope):
    weights = [(1 << 20) // math.isqrt(standing ** slope) + 1 for standing in range(2, count + 1)]
    rest, holding = total - limit - (count - 1), [1] * (count - 1)
    while rest > 0:
        free = [i for i in range(count - 1) if holding[i] < limit]
        mass, remaining = sum([weights[i] for i in free]), rest
        for i in free:
            more = min(limit - holding[i], max(1, remaining * weights[i] // mass), rest)
            holding[i] = holding[i] + more
            rest = rest - more
    return np.array([limit] + holding)


def ragged_sizes(rng, amount, total, most, skew):
    if amount == 2:
        one = jax.random.randint(rng, (), max(1, total - most), min(most, total - 1) + 1)
        return jnp.stack([one, total - one])
    lengths = jnp.asarray(profile(amount, total, most, skew), jnp.int32)
    couples = (amount - 1) // 2
    giver, receiver = lengths[1:1 + 2 * couples:2], lengths[2:2 + 2 * couples:2]
    room = jnp.minimum(giver - 1, most - receiver)
    shifted = jax.random.randint(jax.random.fold_in(rng, 1), (couples,), 0, 1 << 20) % (room + 1)
    lengths = lengths.at[1:1 + 2 * couples:2].set(giver - shifted).at[2:2 + 2 * couples:2].set(receiver + shifted)
    return lengths[jax.random.permutation(jax.random.fold_in(rng, 2), amount)]


def gaussian(rng, dims, scale, limit, pieces=(), kind=jnp.bfloat16):
    result = jax.random.normal(rng, dims, jnp.float32) * scale
    if len(pieces) > 0:
        result = block_levels(rng, dims, pieces, -0.22, 0.18) * result
    return jnp.clip(result, min=-limit, max=limit).astype(kind)


def setup_inputs(seed: int = 0, part: int = 0) -> dict:
    streams_of = jax.random.split(jax.random.key(seed), 11)
    own_keys = jax.random.split(jax.random.fold_in(streams_of[10], part), 11)
    tokens = draw_tokens(jax.random.fold_in(jax.random.fold_in(streams_of[10], part), 71), part)
    weight_query = gaussian(streams_of[1], (D, HEADS * HEAD_DIM), D ** -0.5, 0.046875, ((0, 4), (1, 4)))
    weight_keyval = gaussian(streams_of[2], (D, 2 * KV_HEADS * HEAD_DIM), D ** -0.5, 0.046875, ((0, 4), (1, 4)))
    down_query = gaussian(own_keys[3], (D, RMAX * TENANTS), D ** -0.5, 0.046875, ((0, 4), (1, 4)))
    down_keyval = gaussian(own_keys[4], (D, RMAX * TENANTS), D ** -0.5, 0.046875, ((0, 4), (1, 4)))
    up_query = gaussian(own_keys[5], (RMAX * TENANTS, HEADS * HEAD_DIM), RMAX ** -0.5, 0.5, ((0, 2), (1, 4)))
    up_keyval = gaussian(own_keys[6], (RMAX * TENANTS, 2 * KV_HEADS * HEAD_DIM), RMAX ** -0.5, 0.5, ((0, 2), (1, 4)))
    adapter_rank = draw_adapter_rank(jax.random.fold_in(jax.random.fold_in(streams_of[10], part), 71), part)
    token_lengths = ragged_sizes(own_keys[8], TENANTS, TOKENS, MOST, 2).astype(jnp.int32)
    adapter_slot = jax.random.permutation(own_keys[9], TENANTS).astype(jnp.int32)
    return {"tokens": tokens, "weight_query": weight_query, "weight_keyval": weight_keyval, "down_query": down_query, "down_keyval": down_keyval, "up_query": up_query, "up_keyval": up_keyval, "adapter_rank": adapter_rank, "token_lengths": token_lengths, "adapter_slot": adapter_slot}


ROPE_BASE = 500000.0
ADAPTER_ALPHA = 8.0

def product(left, right):
    return jnp.dot(left, right, preferred_element_type=jnp.float32)

def rotate_pairs(values, position, first_col):
    pair_count = values.shape[1] // 2
    pair_col = first_col + 2 * jnp.arange(pair_count, dtype=jnp.int32)
    within = pair_col % HEAD_DIM // 2
    frequency = jnp.exp(-(2.0 * within.astype(jnp.float32) / HEAD_DIM) * math.log(ROPE_BASE))
    angles = position.astype(jnp.float32)[:, None] * frequency[None, :]
    pair_view = values.reshape(values.shape[0], pair_count, 2)
    even_part = pair_view[:, :, 0]
    odd_part = pair_view[:, :, 1]
    cosine = jnp.cos(angles)
    sine_angle = jnp.sin(angles)
    turned = jnp.stack([even_part * cosine - odd_part * sine_angle, even_part * sine_angle + odd_part * cosine], axis=2)
    return turned.reshape(values.shape)

def tenant_table(token_ids, adapter_rank, token_lengths, adapter_slot):
    segment_ends = jnp.cumsum(token_lengths).astype(jnp.int32)
    begins = segment_ends - token_lengths
    owned_rows = (token_ids[:, None] >= begins[None, :]) & (token_ids[:, None] < segment_ends[None, :])
    zero_int = jnp.zeros((), jnp.int32)
    own_rank = lax.optimization_barrier(jnp.sum(jnp.where(owned_rows, adapter_rank[None, :], zero_int), axis=1))
    own_slot = lax.optimization_barrier(jnp.sum(jnp.where(owned_rows, adapter_slot[None, :], zero_int), axis=1))
    own_first = lax.optimization_barrier(jnp.sum(jnp.where(owned_rows, begins[None, :], zero_int), axis=1))
    slot_hot = own_slot[:, None] == jnp.arange(TENANTS, dtype=jnp.int32)[None, :]
    return (own_rank, own_first, slot_hot)

def select_slot(down_values, slot_hot):
    shaped = down_values.reshape(down_values.shape[0], -1, TENANTS)
    return lax.optimization_barrier(jnp.sum(jnp.where(slot_hot[:, None, :], shaped, 0.0), axis=2))

def scale_ranks(picked, own_rank, first_rank):
    rank_index = first_rank + jnp.arange(picked.shape[1], dtype=jnp.int32)
    keep_mask = rank_index[None, :] < own_rank[:, None]
    factor = ADAPTER_ALPHA / jnp.sqrt(own_rank.astype(jnp.float32))
    return jnp.where(keep_mask, picked * factor[:, None], 0.0).astype(jnp.bfloat16)

def widen_slots(low_values, slot_hot):
    wide_rows = jnp.where(slot_hot[:, None, :], low_values[:, :, None], jnp.zeros((), low_values.dtype))
    return wide_rows.reshape(low_values.shape[0], -1)

def reference(tokens, weight_query, weight_keyval, down_query, down_keyval, up_query, up_keyval, adapter_rank, token_lengths, adapter_slot):
    token_ids = jnp.arange(TOKENS, dtype=jnp.int32)
    own_rank, own_first, slot_hot = tenant_table(token_ids, adapter_rank, token_lengths, adapter_slot)
    position = token_ids - own_first
    proj_query = product(tokens, weight_query)
    proj_keyval = product(tokens, weight_keyval)
    low_query = scale_ranks(select_slot(product(tokens, down_query), slot_hot), own_rank, 0)
    low_keyval = scale_ranks(select_slot(product(tokens, down_keyval), slot_hot), own_rank, 0)
    delta_query = product(widen_slots(low_query, slot_hot), up_query)
    delta_keyval = product(widen_slots(low_keyval, slot_hot), up_keyval)
    query_rows = rotate_pairs(proj_query + delta_query, position, 0).astype(jnp.bfloat16)
    keyval = proj_keyval + delta_keyval
    key_cols = KV_HEADS * HEAD_DIM
    rotated_keys = rotate_pairs(keyval[:, :key_cols], position, 0)
    kv_cache = jnp.concatenate([rotated_keys, keyval[:, key_cols:]], axis=1).astype(jnp.bfloat16)
    group_size = HEADS // KV_HEADS
    visible = (token_ids[None, :] >= own_first[:, None]) & (token_ids[None, :] <= token_ids[:, None])

    def one_head(head_index):
        kv_head = head_index // group_size
        query_head = lax.dynamic_slice_in_dim(query_rows, (head_index * HEAD_DIM).astype(jnp.int32), HEAD_DIM, 1)
        key_head = lax.dynamic_slice_in_dim(kv_cache, (kv_head * HEAD_DIM).astype(jnp.int32), HEAD_DIM, 1)
        value_head = lax.dynamic_slice_in_dim(kv_cache, (key_cols + kv_head * HEAD_DIM).astype(jnp.int32), HEAD_DIM, 1)
        scores = product(query_head, key_head.T) / math.sqrt(HEAD_DIM)
        scores = jnp.where(visible, scores, -1e+30)
        row_top = lax.optimization_barrier(jnp.max(scores, axis=1, keepdims=True))
        exp_scores = jnp.where(visible, jnp.exp(scores - row_top), 0.0)
        attn_weights = exp_scores.astype(jnp.bfloat16)
        summed = product(attn_weights, value_head)
        return (summed / lax.optimization_barrier(jnp.sum(exp_scores, axis=1, keepdims=True))).astype(jnp.bfloat16)
    heads_out = lax.map(one_head, jnp.arange(HEADS, dtype=jnp.int32))
    context = jnp.transpose(heads_out, (1, 0, 2)).reshape(TOKENS, HEADS * HEAD_DIM)
    return (context, kv_cache)
```

```python
import math

import jax
import jax.numpy as jnp
from jax import lax
from jax.sharding import PartitionSpec as P

HEADS = 128
KV_HEADS = 8
HEAD_DIM = 128
TENANTS = 4


ROPE_BASE = 500000.0
ADAPTER_ALPHA = 8.0


def product(left, right):
    return jnp.dot(left, right, preferred_element_type=jnp.float32)


def rotate_pairs(values, position, first_col):
    pair_count = values.shape[1] // 2
    pair_col = first_col + 2 * jnp.arange(pair_count, dtype=jnp.int32)
    within = pair_col % HEAD_DIM // 2
    frequency = jnp.exp(-(2.0 * within.astype(jnp.float32) / HEAD_DIM) * math.log(ROPE_BASE))
    angles = position.astype(jnp.float32)[:, None] * frequency[None, :]
    pair_view = values.reshape(values.shape[0], pair_count, 2)
    even_part = pair_view[:, :, 0]
    odd_part = pair_view[:, :, 1]
    cosine = jnp.cos(angles)
    sine_angle = jnp.sin(angles)
    turned = jnp.stack(
        [even_part * cosine - odd_part * sine_angle, even_part * sine_angle + odd_part * cosine],
        axis=2,
    )
    return turned.reshape(values.shape)


def tenant_table(token_ids, adapter_rank, token_lengths, adapter_slot):
    segment_ends = jnp.cumsum(token_lengths)
    begins = segment_ends - token_lengths
    owned_rows = (token_ids[:, None] >= begins[None, :]) & (
        token_ids[:, None] < segment_ends[None, :]
    )
    zero_int = jnp.zeros((), jnp.int32)
    own_rank = jnp.sum(jnp.where(owned_rows, adapter_rank[None, :], zero_int), axis=1)
    own_slot = jnp.sum(jnp.where(owned_rows, adapter_slot[None, :], zero_int), axis=1)
    own_first = jnp.sum(jnp.where(owned_rows, begins[None, :], zero_int), axis=1)
    slot_hot = own_slot[:, None] == jnp.arange(TENANTS, dtype=jnp.int32)[None, :]
    return (own_rank, own_first, slot_hot)


def select_slot(down_values, slot_hot):
    shaped = down_values.reshape(down_values.shape[0], -1, TENANTS)
    return jnp.sum(jnp.where(slot_hot[:, None, :], shaped, 0.0), axis=2)


def scale_ranks(picked, own_rank, first_rank):
    rank_index = first_rank + jnp.arange(picked.shape[1], dtype=jnp.int32)
    keep_mask = rank_index[None, :] < own_rank[:, None]
    factor = ADAPTER_ALPHA / jnp.sqrt(own_rank.astype(jnp.float32))
    return jnp.where(keep_mask, picked * factor[:, None], 0.0).astype(jnp.bfloat16)


def widen_slots(low_values, slot_hot):
    wide_rows = jnp.where(
        slot_hot[:, None, :], low_values[:, :, None], jnp.zeros((), low_values.dtype)
    )
    return wide_rows.reshape(low_values.shape[0], -1)


def shards(
    tokens,
    weight_query,
    weight_keyval,
    down_query,
    down_keyval,
    up_query,
    up_keyval,
    adapter_rank,
    token_lengths,
    adapter_slot,
):
    ring = lax.axis_size("tensor")
    split = lax.axis_size(("seq", "load"))
    tensor_index = lax.axis_index("tensor")
    block_index = lax.axis_index(("seq", "load"))
    query_cols = weight_query.shape[1]
    keyval_cols = weight_keyval.shape[1]
    rank_share = down_query.shape[1] // TENANTS
    chunk = tokens.shape[0]
    piece = chunk // split
    local_rows = ring * piece

    up_query_all = lax.all_gather(up_query, "load", axis=0, tiled=True)
    up_keyval_all = lax.all_gather(up_keyval, "load", axis=0, tiled=True)

    shift = [(i, (i + 1) % ring) for i in range(ring)]
    held = tokens
    reduced = []
    for step in range(ring):
        following = lax.ppermute(held, "tensor", shift) if step < ring - 1 else None
        owner = (tensor_index - step) % ring
        block_ids = owner * chunk + jnp.arange(chunk, dtype=jnp.int32)
        _, _, block_hot = tenant_table(block_ids, adapter_rank, token_lengths, adapter_slot)
        partial = jnp.concatenate(
            [
                product(held, weight_query),
                product(held, weight_keyval),
                select_slot(product(held, down_query), block_hot),
                select_slot(product(held, down_keyval), block_hot),
            ],
            axis=1,
        )
        reduced.append(
            lax.psum_scatter(partial, ("seq", "load"), scatter_dimension=0, tiled=True)
        )
        held = following
    steps_of_owner = (tensor_index - jnp.arange(ring, dtype=jnp.int32)) % ring
    summed = jnp.take(jnp.stack(reduced), steps_of_owner, axis=0).reshape(local_rows, -1)

    owners = jnp.arange(ring, dtype=jnp.int32)
    piece_ids = jnp.arange(piece, dtype=jnp.int32)
    token_ids = (owners[:, None] * chunk + block_index * piece + piece_ids[None, :]).reshape(-1)
    own_rank, own_first, slot_hot = tenant_table(
        token_ids, adapter_rank, token_lengths, adapter_slot
    )
    position = token_ids - own_first
    low_start = query_cols + keyval_cols
    first_rank = tensor_index * rank_share
    low_query = scale_ranks(summed[:, low_start : low_start + rank_share], own_rank, first_rank)
    low_keyval = scale_ranks(summed[:, low_start + rank_share :], own_rank, first_rank)
    low_both = lax.all_gather(
        jnp.concatenate([low_query, low_keyval], axis=1), "tensor", axis=1
    )
    full_query = low_both[:, :, :rank_share].reshape(local_rows, -1)
    full_keyval = low_both[:, :, rank_share:].reshape(local_rows, -1)
    wide_query = widen_slots(full_query, slot_hot)
    wide_keyval = widen_slots(full_keyval, slot_hot)
    delta_query = product(wide_query, up_query_all)
    delta_keyval = product(wide_keyval, up_keyval_all)
    query_rows = rotate_pairs(
        summed[:, :query_cols] + delta_query, position, tensor_index * query_cols
    ).astype(jnp.bfloat16)
    keyval = summed[:, query_cols:low_start] + delta_keyval
    kv_first_col = tensor_index * keyval_cols
    is_key = kv_first_col + jnp.arange(keyval_cols, dtype=jnp.int32) < KV_HEADS * HEAD_DIM
    kv_local = jnp.where(
        is_key[None, :], rotate_pairs(keyval, position, kv_first_col), keyval
    ).astype(jnp.bfloat16)
    kv_all = lax.all_gather(kv_local, "tensor", axis=1, tiled=True)
    heads_here = query_cols // HEAD_DIM
    group_size = HEADS // KV_HEADS
    kv_here = max(heads_here // group_size, 1)
    per_kv = heads_here // kv_here
    kv_first = tensor_index * heads_here // group_size
    key_cols = KV_HEADS * HEAD_DIM
    key_heads = lax.dynamic_slice_in_dim(
        kv_all, kv_first * HEAD_DIM, kv_here * HEAD_DIM, 1
    ).reshape(local_rows, kv_here, HEAD_DIM)
    value_heads = lax.dynamic_slice_in_dim(
        kv_all, key_cols + kv_first * HEAD_DIM, kv_here * HEAD_DIM, 1
    ).reshape(local_rows, kv_here, HEAD_DIM)
    both_heads = lax.all_gather(
        jnp.concatenate([key_heads, value_heads], axis=1), ("seq", "load"), axis=0, tiled=True
    )
    piece_keys = both_heads[:, :kv_here]
    piece_values = both_heads[:, kv_here:]
    key_ids = (
        owners[None, :, None] * chunk
        + jnp.arange(split, dtype=jnp.int32)[:, None, None] * piece
        + piece_ids[None, None, :]
    ).reshape(-1)
    grouped = query_rows.reshape(local_rows, kv_here, per_kv, HEAD_DIM)
    visible = (key_ids[None, :] >= own_first[:, None]) & (key_ids[None, :] <= token_ids[:, None])
    scores = jnp.einsum(
        "qghd,kgd->ghqk", grouped, piece_keys, preferred_element_type=jnp.float32
    ) / math.sqrt(HEAD_DIM)
    scores = jnp.where(visible, scores, -1e30)
    row_top = jnp.max(scores, axis=3)
    exp_scores = jnp.where(visible, jnp.exp(scores - row_top[..., None]), 0.0)
    row_total = jnp.sum(exp_scores, axis=3)
    accumulated = jnp.einsum(
        "ghqk,kgd->ghqd",
        exp_scores.astype(jnp.bfloat16),
        piece_values,
        preferred_element_type=jnp.float32,
    )
    context = (accumulated / row_total[..., None]).astype(jnp.bfloat16)
    context = jnp.transpose(context, (2, 0, 1, 3)).reshape(local_rows, query_cols)

    outgoing = jnp.concatenate([context, kv_local], axis=1)
    by_owner = outgoing.reshape(split, ring // split, piece, -1)
    arrived = lax.all_to_all(by_owner, ("seq", "load"), 0, 0)
    placed = jnp.transpose(arrived, (1, 0, 2, 3)).reshape(local_rows, -1)
    return (placed[:, :query_cols], placed[:, query_cols:])


def solution(mesh):
    placed = (
        P(("groups", "tensor"), ("seq", "load")),
        P(("seq", "load"), "tensor"),
        P(("seq", "load"), "tensor"),
        P(("seq", "load"), ("groups", "tensor")),
        P(("seq", "load"), ("groups", "tensor")),
        P(("groups", "load"), "tensor"),
        P(("groups", "load"), "tensor"),
        P("groups"),
        P("groups"),
        P("groups"),
    )
    return jax.shard_map(
        shards,
        mesh=mesh,
        in_specs=placed,
        out_specs=(P(("groups", "seq", "load"), "tensor"), P(("groups", "seq", "load"), "tensor")),
        check_vma=False,
    )
```

```python
import math

import jax
import jax.numpy as jnp
from jax import lax
from jax.sharding import PartitionSpec as P

HEADS = 128
KV_HEADS = 8
HEAD_DIM = 128
TENANTS = 4


ROPE_BASE = 500000.0
ADAPTER_ALPHA = 8.0


def product(left, right):
    return jnp.dot(left, right, preferred_element_type=jnp.float32)


def rotate_pairs(values, position, first_col):
    pair_count = values.shape[1] // 2
    pair_col = first_col + 2 * jnp.arange(pair_count, dtype=jnp.int32)
    within = pair_col % HEAD_DIM // 2
    frequency = jnp.exp(-(2.0 * within.astype(jnp.float32) / HEAD_DIM) * math.log(ROPE_BASE))
    angles = position.astype(jnp.float32)[:, None] * frequency[None, :]
    pair_view = values.reshape(values.shape[0], pair_count, 2)
    even_part = pair_view[:, :, 0]
    odd_part = pair_view[:, :, 1]
    cosine = jnp.cos(angles)
    sine_angle = jnp.sin(angles)
    turned = jnp.stack(
        [even_part * cosine - odd_part * sine_angle, even_part * sine_angle + odd_part * cosine],
        axis=2,
    )
    return turned.reshape(values.shape)


def tenant_table(token_ids, adapter_rank, token_lengths, adapter_slot):
    segment_ends = jnp.cumsum(token_lengths)
    begins = segment_ends - token_lengths
    owned_rows = (token_ids[:, None] >= begins[None, :]) & (
        token_ids[:, None] < segment_ends[None, :]
    )
    zero_int = jnp.zeros((), jnp.int32)
    own_rank = jnp.sum(jnp.where(owned_rows, adapter_rank[None, :], zero_int), axis=1)
    own_slot = jnp.sum(jnp.where(owned_rows, adapter_slot[None, :], zero_int), axis=1)
    own_first = jnp.sum(jnp.where(owned_rows, begins[None, :], zero_int), axis=1)
    slot_hot = own_slot[:, None] == jnp.arange(TENANTS, dtype=jnp.int32)[None, :]
    return (own_rank, own_first, slot_hot)


def select_slot(down_values, slot_hot):
    shaped = down_values.reshape(down_values.shape[0], -1, TENANTS)
    return jnp.sum(jnp.where(slot_hot[:, None, :], shaped, 0.0), axis=2)


def scale_ranks(picked, own_rank, first_rank):
    rank_index = first_rank + jnp.arange(picked.shape[1], dtype=jnp.int32)
    keep_mask = rank_index[None, :] < own_rank[:, None]
    factor = ADAPTER_ALPHA / jnp.sqrt(own_rank.astype(jnp.float32))
    return jnp.where(keep_mask, picked * factor[:, None], 0.0).astype(jnp.bfloat16)


def widen_slots(low_values, slot_hot):
    wide_rows = jnp.where(
        slot_hot[:, None, :], low_values[:, :, None], jnp.zeros((), low_values.dtype)
    )
    return wide_rows.reshape(low_values.shape[0], -1)


def shards(
    tokens,
    weight_query,
    weight_keyval,
    down_query,
    down_keyval,
    up_query,
    up_keyval,
    adapter_rank,
    token_lengths,
    adapter_slot,
):
    tensor_count = lax.axis_size("tensor")
    block_count = lax.axis_size(("seq", "load"))
    tensor_index = lax.axis_index("tensor")
    block_index = lax.axis_index(("seq", "load"))
    query_cols = weight_query.shape[1]
    keyval_cols = weight_keyval.shape[1]
    rank_share = down_query.shape[1] // TENANTS
    block_rows = tokens.shape[0] * tensor_count // block_count
    up_query_all = lax.all_gather(up_query, "load", axis=0, tiled=True)
    up_keyval_all = lax.all_gather(up_keyval, "load", axis=0, tiled=True)
    shard_rows = lax.all_gather(tokens, "tensor", axis=0, tiled=True)
    piece_ids = jnp.arange(shard_rows.shape[0], dtype=jnp.int32)
    piece_rank, piece_first, piece_hot = tenant_table(
        piece_ids, adapter_rank, token_lengths, adapter_slot
    )
    small_terms = jnp.concatenate(
        [
            product(shard_rows, weight_keyval),
            select_slot(product(shard_rows, down_query), piece_hot),
            select_slot(product(shard_rows, down_keyval), piece_hot),
        ],
        axis=1,
    )
    small_summed = lax.psum_scatter(small_terms, ("seq", "load"), scatter_dimension=0, tiled=True)
    query_summed = lax.psum_scatter(
        product(shard_rows, weight_query), ("seq", "load"), scatter_dimension=0, tiled=True
    )
    token_ids = block_index * block_rows + jnp.arange(block_rows, dtype=jnp.int32)
    own_rank, own_first, slot_hot = tenant_table(
        token_ids, adapter_rank, token_lengths, adapter_slot
    )
    position = token_ids - own_first
    first_rank = tensor_index * rank_share
    low_query = scale_ranks(
        small_summed[:, keyval_cols : keyval_cols + rank_share], own_rank, first_rank
    )
    low_keyval = scale_ranks(small_summed[:, keyval_cols + rank_share :], own_rank, first_rank)
    low_both = lax.all_gather(
        jnp.concatenate([low_query, low_keyval], axis=1), "tensor", axis=1
    )
    full_query = low_both[:, :, :rank_share].reshape(block_rows, -1)
    full_keyval = low_both[:, :, rank_share:].reshape(block_rows, -1)
    wide_query = widen_slots(full_query, slot_hot)
    wide_keyval = widen_slots(full_keyval, slot_hot)
    delta_keyval = product(wide_keyval, up_keyval_all)
    keyval = small_summed[:, :keyval_cols] + delta_keyval
    kv_first_col = tensor_index * keyval_cols
    is_key = kv_first_col + jnp.arange(keyval_cols, dtype=jnp.int32) < KV_HEADS * HEAD_DIM
    kv_local = jnp.where(
        is_key[None, :], rotate_pairs(keyval, position, kv_first_col), keyval
    ).astype(jnp.bfloat16)
    kv_all = lax.all_gather(kv_local, "tensor", axis=1, tiled=True)
    heads_here = query_cols // HEAD_DIM
    group_size = HEADS // KV_HEADS
    kv_here = max(heads_here // group_size, 1)
    per_kv = heads_here // kv_here
    kv_first = tensor_index * heads_here // group_size
    key_cols = KV_HEADS * HEAD_DIM
    key_heads = lax.dynamic_slice_in_dim(
        kv_all, kv_first * HEAD_DIM, kv_here * HEAD_DIM, 1
    ).reshape(block_rows, kv_here, HEAD_DIM)
    value_heads = lax.dynamic_slice_in_dim(
        kv_all, key_cols + kv_first * HEAD_DIM, kv_here * HEAD_DIM, 1
    ).reshape(block_rows, kv_here, HEAD_DIM)
    both_heads = lax.all_gather(
        jnp.concatenate([key_heads, value_heads], axis=1), ("seq", "load"), axis=0, tiled=True
    )
    piece_keys = both_heads[:, :kv_here]
    piece_values = both_heads[:, kv_here:]
    delta_query = product(wide_query, up_query_all)
    query_rows = rotate_pairs(
        query_summed + delta_query, position, tensor_index * query_cols
    ).astype(jnp.bfloat16)
    grouped = query_rows.reshape(block_rows, kv_here, per_kv, HEAD_DIM)
    key_ids = jnp.arange(piece_keys.shape[0], dtype=jnp.int32)
    visible = (key_ids[None, :] >= own_first[:, None]) & (key_ids[None, :] <= token_ids[:, None])
    scores = jnp.einsum(
        "qghd,kgd->ghqk", grouped, piece_keys, preferred_element_type=jnp.float32
    ) / math.sqrt(HEAD_DIM)
    scores = jnp.where(visible, scores, -1e30)
    row_top = jnp.max(scores, axis=3)
    exp_scores = jnp.where(visible, jnp.exp(scores - row_top[..., None]), 0.0)
    row_total = jnp.sum(exp_scores, axis=3)
    accumulated = jnp.einsum(
        "ghqk,kgd->ghqd",
        exp_scores.astype(jnp.bfloat16),
        piece_values,
        preferred_element_type=jnp.float32,
    )
    context = (accumulated / row_total[..., None]).astype(jnp.bfloat16)
    context = jnp.transpose(context, (2, 0, 1, 3)).reshape(block_rows, query_cols)
    return (context, kv_local)


def solution(mesh):
    placed = (
        P(("groups", "tensor"), ("seq", "load")),
        P(("seq", "load"), "tensor"),
        P(("seq", "load"), "tensor"),
        P(("seq", "load"), ("groups", "tensor")),
        P(("seq", "load"), ("groups", "tensor")),
        P(("groups", "load"), "tensor"),
        P(("groups", "load"), "tensor"),
        P("groups"),
        P("groups"),
        P("groups"),
    )
    return jax.shard_map(
        shards,
        mesh=mesh,
        in_specs=placed,
        out_specs=(P(("groups", "seq", "load"), "tensor"), P(("groups", "seq", "load"), "tensor")),
        check_vma=False,
    )
```

```python
import math

import jax
import jax.numpy as jnp
from jax import lax
from jax.sharding import PartitionSpec as P

HEADS = 128
KV_HEADS = 8
HEAD_DIM = 128
TENANTS = 4


ROPE_BASE = 500000.0
ADAPTER_ALPHA = 8.0


def product(left, right):
    return jnp.dot(left, right, preferred_element_type=jnp.float32)


def rotate_pairs(values, position, first_col):
    pair_count = values.shape[1] // 2
    pair_col = first_col + 2 * jnp.arange(pair_count, dtype=jnp.int32)
    within = pair_col % HEAD_DIM // 2
    frequency = jnp.exp(-(2.0 * within.astype(jnp.float32) / HEAD_DIM) * math.log(ROPE_BASE))
    angles = position.astype(jnp.float32)[:, None] * frequency[None, :]
    pair_view = values.reshape(values.shape[0], pair_count, 2)
    even_part = pair_view[:, :, 0]
    odd_part = pair_view[:, :, 1]
    cosine = jnp.cos(angles)
    sine_angle = jnp.sin(angles)
    turned = jnp.stack(
        [even_part * cosine - odd_part * sine_angle, even_part * sine_angle + odd_part * cosine],
        axis=2,
    )
    return turned.reshape(values.shape)


def tenant_table(token_ids, adapter_rank, token_lengths, adapter_slot):
    segment_ends = jnp.cumsum(token_lengths)
    begins = segment_ends - token_lengths
    owned_rows = (token_ids[:, None] >= begins[None, :]) & (
        token_ids[:, None] < segment_ends[None, :]
    )
    zero_int = jnp.zeros((), jnp.int32)
    own_rank = jnp.sum(jnp.where(owned_rows, adapter_rank[None, :], zero_int), axis=1)
    own_slot = jnp.sum(jnp.where(owned_rows, adapter_slot[None, :], zero_int), axis=1)
    own_first = jnp.sum(jnp.where(owned_rows, begins[None, :], zero_int), axis=1)
    slot_hot = own_slot[:, None] == jnp.arange(TENANTS, dtype=jnp.int32)[None, :]
    return (own_rank, own_first, slot_hot)


def select_slot(down_values, slot_hot):
    shaped = down_values.reshape(down_values.shape[0], -1, TENANTS)
    return jnp.sum(jnp.where(slot_hot[:, None, :], shaped, 0.0), axis=2)


def scale_ranks(picked, own_rank, first_rank):
    rank_index = first_rank + jnp.arange(picked.shape[1], dtype=jnp.int32)
    keep_mask = rank_index[None, :] < own_rank[:, None]
    factor = ADAPTER_ALPHA / jnp.sqrt(own_rank.astype(jnp.float32))
    return jnp.where(keep_mask, picked * factor[:, None], 0.0).astype(jnp.bfloat16)


def widen_slots(low_values, slot_hot):
    wide_rows = jnp.where(
        slot_hot[:, None, :], low_values[:, :, None], jnp.zeros((), low_values.dtype)
    )
    return wide_rows.reshape(low_values.shape[0], -1)


def shards(
    tokens,
    weight_query,
    weight_keyval,
    down_query,
    down_keyval,
    up_query,
    up_keyval,
    adapter_rank,
    token_lengths,
    adapter_slot,
):
    tensor_count = lax.axis_size("tensor")
    block_count = lax.axis_size(("seq", "load"))
    tensor_index = lax.axis_index("tensor")
    block_index = lax.axis_index(("seq", "load"))
    query_cols = weight_query.shape[1]
    keyval_cols = weight_keyval.shape[1]
    rank_share = down_query.shape[1] // TENANTS
    block_rows = tokens.shape[0] * tensor_count // block_count
    up_query_all = lax.all_gather(up_query, "load", axis=0, tiled=True)
    up_keyval_all = lax.all_gather(up_keyval, "load", axis=0, tiled=True)
    shard_rows = lax.all_gather(tokens, "tensor", axis=0, tiled=True)
    piece_ids = jnp.arange(shard_rows.shape[0], dtype=jnp.int32)
    piece_rank, piece_first, piece_hot = tenant_table(
        piece_ids, adapter_rank, token_lengths, adapter_slot
    )
    small_terms = jnp.concatenate(
        [
            product(shard_rows, weight_keyval),
            select_slot(product(shard_rows, down_query), piece_hot),
            select_slot(product(shard_rows, down_keyval), piece_hot),
        ],
        axis=1,
    )
    small_summed = lax.psum_scatter(small_terms, ("seq", "load"), scatter_dimension=0, tiled=True)
    seq_count = lax.axis_size("seq")
    load_count = lax.axis_size("load")
    by_core = shard_rows.reshape(seq_count, load_count, block_rows, -1)
    core_terms = jnp.stack(
        [
            product(by_core[:, core].reshape(seq_count * block_rows, -1), weight_query)
            for core in range(load_count)
        ]
    )
    core_summed = lax.psum_scatter(core_terms, "load", scatter_dimension=0, tiled=True)
    query_summed = lax.psum_scatter(
        core_summed.reshape(seq_count * block_rows, -1), "seq", scatter_dimension=0, tiled=True
    )
    token_ids = block_index * block_rows + jnp.arange(block_rows, dtype=jnp.int32)
    own_rank, own_first, slot_hot = tenant_table(
        token_ids, adapter_rank, token_lengths, adapter_slot
    )
    position = token_ids - own_first
    first_rank = tensor_index * rank_share
    low_query = scale_ranks(
        small_summed[:, keyval_cols : keyval_cols + rank_share], own_rank, first_rank
    )
    low_keyval = scale_ranks(small_summed[:, keyval_cols + rank_share :], own_rank, first_rank)
    low_both = lax.all_gather(
        jnp.concatenate([low_query, low_keyval], axis=1), "tensor", axis=1
    )
    full_query = low_both[:, :, :rank_share].reshape(block_rows, -1)
    full_keyval = low_both[:, :, rank_share:].reshape(block_rows, -1)
    wide_query = widen_slots(full_query, slot_hot)
    wide_keyval = widen_slots(full_keyval, slot_hot)
    delta_keyval = product(wide_keyval, up_keyval_all)
    keyval = small_summed[:, :keyval_cols] + delta_keyval
    kv_first_col = tensor_index * keyval_cols
    is_key = kv_first_col + jnp.arange(keyval_cols, dtype=jnp.int32) < KV_HEADS * HEAD_DIM
    kv_local = jnp.where(
        is_key[None, :], rotate_pairs(keyval, position, kv_first_col), keyval
    ).astype(jnp.bfloat16)
    kv_all = lax.all_gather(kv_local, "tensor", axis=1, tiled=True)
    heads_here = query_cols // HEAD_DIM
    group_size = HEADS // KV_HEADS
    kv_here = max(heads_here // group_size, 1)
    per_kv = heads_here // kv_here
    kv_first = tensor_index * heads_here // group_size
    key_cols = KV_HEADS * HEAD_DIM
    key_heads = lax.dynamic_slice_in_dim(
        kv_all, kv_first * HEAD_DIM, kv_here * HEAD_DIM, 1
    ).reshape(block_rows, kv_here, HEAD_DIM)
    value_heads = lax.dynamic_slice_in_dim(
        kv_all, key_cols + kv_first * HEAD_DIM, kv_here * HEAD_DIM, 1
    ).reshape(block_rows, kv_here, HEAD_DIM)
    both_heads = lax.all_gather(
        jnp.concatenate([key_heads, value_heads], axis=1), ("seq", "load"), axis=0, tiled=True
    )
    piece_keys = both_heads[:, :kv_here]
    piece_values = both_heads[:, kv_here:]
    delta_query = lax.optimization_barrier(product(wide_query, up_query_all))
    query_rows = rotate_pairs(
        query_summed + delta_query, position, tensor_index * query_cols
    ).astype(jnp.bfloat16)
    grouped = query_rows.reshape(block_rows, kv_here, per_kv, HEAD_DIM)
    key_ids = jnp.arange(piece_keys.shape[0], dtype=jnp.int32)
    visible = (key_ids[None, :] >= own_first[:, None]) & (key_ids[None, :] <= token_ids[:, None])
    scores = jnp.einsum(
        "qghd,kgd->ghqk", grouped, piece_keys, preferred_element_type=jnp.float32
    ) / math.sqrt(HEAD_DIM)
    scores = jnp.where(visible, scores, -1e30)
    row_top = jnp.max(scores, axis=3)
    exp_scores = jnp.where(visible, jnp.exp(scores - row_top[..., None]), 0.0)
    row_total = jnp.sum(exp_scores, axis=3)
    accumulated = jnp.einsum(
        "ghqk,kgd->ghqd",
        exp_scores.astype(jnp.bfloat16),
        piece_values,
        preferred_element_type=jnp.float32,
    )
    context = (accumulated / row_total[..., None]).astype(jnp.bfloat16)
    context = jnp.transpose(context, (2, 0, 1, 3)).reshape(block_rows, query_cols)
    return (context, kv_local)


def solution(mesh):
    placed = (
        P(("groups", "tensor"), ("seq", "load")),
        P(("seq", "load"), "tensor"),
        P(("seq", "load"), "tensor"),
        P(("seq", "load"), ("groups", "tensor")),
        P(("seq", "load"), ("groups", "tensor")),
        P(("groups", "load"), "tensor"),
        P(("groups", "load"), "tensor"),
        P("groups"),
        P("groups"),
        P("groups"),
    )
    return jax.shard_map(
        shards,
        mesh=mesh,
        in_specs=placed,
        out_specs=(P(("groups", "seq", "load"), "tensor"), P(("groups", "seq", "load"), "tensor")),
        check_vma=False,
    )
```

```python
import math

import jax
import jax.numpy as jnp
from jax import lax
from jax.sharding import PartitionSpec as P

HEADS = 128
KV_HEADS = 8
HEAD_DIM = 128
TENANTS = 4


ROPE_BASE = 500000.0
ADAPTER_ALPHA = 8.0


def product(left, right):
    return jnp.dot(left, right, preferred_element_type=jnp.float32)


def rotate_pairs(values, position, first_col):
    pair_count = values.shape[1] // 2
    pair_col = first_col + 2 * jnp.arange(pair_count, dtype=jnp.int32)
    within = pair_col % HEAD_DIM // 2
    frequency = jnp.exp(-(2.0 * within.astype(jnp.float32) / HEAD_DIM) * math.log(ROPE_BASE))
    angles = position.astype(jnp.float32)[:, None] * frequency[None, :]
    pair_view = values.reshape(values.shape[0], pair_count, 2)
    even_part = pair_view[:, :, 0]
    odd_part = pair_view[:, :, 1]
    cosine = jnp.cos(angles)
    sine_angle = jnp.sin(angles)
    turned = jnp.stack(
        [even_part * cosine - odd_part * sine_angle, even_part * sine_angle + odd_part * cosine],
        axis=2,
    )
    return turned.reshape(values.shape)


def tenant_table(token_ids, adapter_rank, token_lengths, adapter_slot):
    segment_ends = jnp.cumsum(token_lengths)
    begins = segment_ends - token_lengths
    owned_rows = (token_ids[:, None] >= begins[None, :]) & (
        token_ids[:, None] < segment_ends[None, :]
    )
    zero_int = jnp.zeros((), jnp.int32)
    own_rank = jnp.sum(jnp.where(owned_rows, adapter_rank[None, :], zero_int), axis=1)
    own_slot = jnp.sum(jnp.where(owned_rows, adapter_slot[None, :], zero_int), axis=1)
    own_first = jnp.sum(jnp.where(owned_rows, begins[None, :], zero_int), axis=1)
    slot_hot = own_slot[:, None] == jnp.arange(TENANTS, dtype=jnp.int32)[None, :]
    return (own_rank, own_first, slot_hot)


def select_slot(down_values, slot_hot):
    shaped = down_values.reshape(down_values.shape[0], -1, TENANTS)
    return jnp.sum(jnp.where(slot_hot[:, None, :], shaped, 0.0), axis=2)


def scale_ranks(picked, own_rank, first_rank):
    rank_index = first_rank + jnp.arange(picked.shape[1], dtype=jnp.int32)
    keep_mask = rank_index[None, :] < own_rank[:, None]
    factor = ADAPTER_ALPHA / jnp.sqrt(own_rank.astype(jnp.float32))
    return jnp.where(keep_mask, picked * factor[:, None], 0.0).astype(jnp.bfloat16)


def widen_slots(low_values, slot_hot):
    wide_rows = jnp.where(
        slot_hot[:, None, :], low_values[:, :, None], jnp.zeros((), low_values.dtype)
    )
    return wide_rows.reshape(low_values.shape[0], -1)


def shards(
    tokens,
    weight_query,
    weight_keyval,
    down_query,
    down_keyval,
    up_query,
    up_keyval,
    adapter_rank,
    token_lengths,
    adapter_slot,
):
    tensor_count = lax.axis_size("tensor")
    block_count = lax.axis_size(("seq", "load"))
    tensor_index = lax.axis_index("tensor")
    block_index = lax.axis_index(("seq", "load"))
    query_cols = weight_query.shape[1]
    keyval_cols = weight_keyval.shape[1]
    rank_share = down_query.shape[1] // TENANTS
    block_rows = tokens.shape[0] * tensor_count // block_count
    up_query_all = lax.all_gather(up_query, "load", axis=0, tiled=True)
    up_keyval_all = lax.all_gather(up_keyval, "load", axis=0, tiled=True)
    piece_ids = jnp.arange(tokens.shape[0] * tensor_count, dtype=jnp.int32)
    piece_rank, piece_first, piece_hot = tenant_table(
        piece_ids, adapter_rank, token_lengths, adapter_slot
    )
    halves = 2
    half = tokens.shape[1] // halves
    gathered = [
        lax.all_gather(tokens[:, part * half : (part + 1) * half], "tensor", axis=0, tiled=True)
        for part in range(halves)
    ]
    small_terms = None
    query_terms = None
    for part in range(halves):
        rows_part = gathered[part]
        if small_terms is not None:
            rows_part, small_terms, query_terms = lax.optimization_barrier(
                (rows_part, small_terms, query_terms)
            )
        feats = slice(part * half, (part + 1) * half)
        small_part = jnp.concatenate(
            [
                product(rows_part, weight_keyval[feats]),
                select_slot(product(rows_part, down_query[feats]), piece_hot),
                select_slot(product(rows_part, down_keyval[feats]), piece_hot),
            ],
            axis=1,
        )
        query_part = product(rows_part, weight_query[feats])
        small_terms = small_part if small_terms is None else small_terms + small_part
        query_terms = query_part if query_terms is None else query_terms + query_part
    small_summed = lax.psum_scatter(small_terms, ("seq", "load"), scatter_dimension=0, tiled=True)
    query_summed = lax.psum_scatter(query_terms, ("seq", "load"), scatter_dimension=0, tiled=True)
    token_ids = block_index * block_rows + jnp.arange(block_rows, dtype=jnp.int32)
    own_rank, own_first, slot_hot = tenant_table(
        token_ids, adapter_rank, token_lengths, adapter_slot
    )
    position = token_ids - own_first
    first_rank = tensor_index * rank_share
    low_query = scale_ranks(
        small_summed[:, keyval_cols : keyval_cols + rank_share], own_rank, first_rank
    )
    low_keyval = scale_ranks(small_summed[:, keyval_cols + rank_share :], own_rank, first_rank)
    low_both = lax.all_gather(
        jnp.concatenate([low_query, low_keyval], axis=1), "tensor", axis=1
    )
    full_query = low_both[:, :, :rank_share].reshape(block_rows, -1)
    full_keyval = low_both[:, :, rank_share:].reshape(block_rows, -1)
    wide_query = widen_slots(full_query, slot_hot)
    wide_keyval = widen_slots(full_keyval, slot_hot)
    delta_keyval = product(wide_keyval, up_keyval_all)
    keyval = small_summed[:, :keyval_cols] + delta_keyval
    kv_first_col = tensor_index * keyval_cols
    is_key = kv_first_col + jnp.arange(keyval_cols, dtype=jnp.int32) < KV_HEADS * HEAD_DIM
    kv_local = jnp.where(
        is_key[None, :], rotate_pairs(keyval, position, kv_first_col), keyval
    ).astype(jnp.bfloat16)
    kv_all = lax.all_gather(kv_local, "tensor", axis=1, tiled=True)
    heads_here = query_cols // HEAD_DIM
    group_size = HEADS // KV_HEADS
    kv_here = max(heads_here // group_size, 1)
    per_kv = heads_here // kv_here
    kv_first = tensor_index * heads_here // group_size
    key_cols = KV_HEADS * HEAD_DIM
    key_heads = lax.dynamic_slice_in_dim(
        kv_all, kv_first * HEAD_DIM, kv_here * HEAD_DIM, 1
    ).reshape(block_rows, kv_here, HEAD_DIM)
    value_heads = lax.dynamic_slice_in_dim(
        kv_all, key_cols + kv_first * HEAD_DIM, kv_here * HEAD_DIM, 1
    ).reshape(block_rows, kv_here, HEAD_DIM)
    both_heads = lax.all_gather(
        jnp.concatenate([key_heads, value_heads], axis=1), ("seq", "load"), axis=0, tiled=True
    )
    piece_keys = both_heads[:, :kv_here]
    piece_values = both_heads[:, kv_here:]
    delta_query = lax.optimization_barrier(product(wide_query, up_query_all))
    query_rows = rotate_pairs(
        query_summed + delta_query, position, tensor_index * query_cols
    ).astype(jnp.bfloat16)
    grouped = query_rows.reshape(block_rows, kv_here, per_kv, HEAD_DIM)
    key_ids = jnp.arange(piece_keys.shape[0], dtype=jnp.int32)
    visible = (key_ids[None, :] >= own_first[:, None]) & (key_ids[None, :] <= token_ids[:, None])
    scores = jnp.einsum(
        "qghd,kgd->ghqk", grouped, piece_keys, preferred_element_type=jnp.float32
    ) / math.sqrt(HEAD_DIM)
    scores = jnp.where(visible, scores, -1e30)
    row_top = jnp.max(scores, axis=3)
    exp_scores = jnp.where(visible, jnp.exp(scores - row_top[..., None]), 0.0)
    row_total = jnp.sum(exp_scores, axis=3)
    accumulated = jnp.einsum(
        "ghqk,kgd->ghqd",
        exp_scores.astype(jnp.bfloat16),
        piece_values,
        preferred_element_type=jnp.float32,
    )
    context = (accumulated / row_total[..., None]).astype(jnp.bfloat16)
    context = jnp.transpose(context, (2, 0, 1, 3)).reshape(block_rows, query_cols)
    return (context, kv_local)


def solution(mesh):
    placed = (
        P(("groups", "tensor"), ("seq", "load")),
        P(("seq", "load"), "tensor"),
        P(("seq", "load"), "tensor"),
        P(("seq", "load"), ("groups", "tensor")),
        P(("seq", "load"), ("groups", "tensor")),
        P(("groups", "load"), "tensor"),
        P(("groups", "load"), "tensor"),
        P("groups"),
        P("groups"),
        P("groups"),
    )
    return jax.shard_map(
        shards,
        mesh=mesh,
        in_specs=placed,
        out_specs=(P(("groups", "seq", "load"), "tensor"), P(("groups", "seq", "load"), "tensor")),
        check_vma=False,
    )
```

```python
import math

import jax
import jax.numpy as jnp
from jax import lax
from jax.sharding import PartitionSpec as P

HEADS = 128
KV_HEADS = 8
HEAD_DIM = 128
TENANTS = 4


ROPE_BASE = 500000.0
ADAPTER_ALPHA = 8.0


def product(left, right):
    return jnp.dot(left, right, preferred_element_type=jnp.float32)


def rotate_pairs(values, position, first_col):
    pair_count = values.shape[1] // 2
    pair_col = first_col + 2 * jnp.arange(pair_count, dtype=jnp.int32)
    within = pair_col % HEAD_DIM // 2
    frequency = jnp.exp(-(2.0 * within.astype(jnp.float32) / HEAD_DIM) * math.log(ROPE_BASE))
    angles = position.astype(jnp.float32)[:, None] * frequency[None, :]
    pair_view = values.reshape(values.shape[0], pair_count, 2)
    even_part = pair_view[:, :, 0]
    odd_part = pair_view[:, :, 1]
    cosine = jnp.cos(angles)
    sine_angle = jnp.sin(angles)
    turned = jnp.stack(
        [even_part * cosine - odd_part * sine_angle, even_part * sine_angle + odd_part * cosine],
        axis=2,
    )
    return turned.reshape(values.shape)


def tenant_table(token_ids, adapter_rank, token_lengths, adapter_slot):
    segment_ends = jnp.cumsum(token_lengths)
    begins = segment_ends - token_lengths
    owned_rows = (token_ids[:, None] >= begins[None, :]) & (
        token_ids[:, None] < segment_ends[None, :]
    )
    zero_int = jnp.zeros((), jnp.int32)
    own_rank = jnp.sum(jnp.where(owned_rows, adapter_rank[None, :], zero_int), axis=1)
    own_slot = jnp.sum(jnp.where(owned_rows, adapter_slot[None, :], zero_int), axis=1)
    own_first = jnp.sum(jnp.where(owned_rows, begins[None, :], zero_int), axis=1)
    slot_hot = own_slot[:, None] == jnp.arange(TENANTS, dtype=jnp.int32)[None, :]
    return (own_rank, own_first, slot_hot)


def select_slot(down_values, slot_hot):
    shaped = down_values.reshape(down_values.shape[0], -1, TENANTS)
    return jnp.sum(jnp.where(slot_hot[:, None, :], shaped, 0.0), axis=2)


def scale_ranks(picked, own_rank, first_rank):
    rank_index = first_rank + jnp.arange(picked.shape[1], dtype=jnp.int32)
    keep_mask = rank_index[None, :] < own_rank[:, None]
    factor = ADAPTER_ALPHA / jnp.sqrt(own_rank.astype(jnp.float32))
    return jnp.where(keep_mask, picked * factor[:, None], 0.0).astype(jnp.bfloat16)


def widen_slots(low_values, slot_hot):
    wide_rows = jnp.where(
        slot_hot[:, None, :], low_values[:, :, None], jnp.zeros((), low_values.dtype)
    )
    return wide_rows.reshape(low_values.shape[0], -1)


def shards(
    tokens,
    weight_query,
    weight_keyval,
    down_query,
    down_keyval,
    up_query,
    up_keyval,
    adapter_rank,
    token_lengths,
    adapter_slot,
):
    tensor_count = lax.axis_size("tensor")
    block_count = lax.axis_size(("seq", "load"))
    tensor_index = lax.axis_index("tensor")
    block_index = lax.axis_index(("seq", "load"))
    query_cols = weight_query.shape[1]
    keyval_cols = weight_keyval.shape[1]
    rank_share = down_query.shape[1] // TENANTS
    block_rows = tokens.shape[0] * tensor_count // block_count
    up_query_all = lax.all_gather(up_query, "load", axis=0, tiled=True)
    up_keyval_all = lax.all_gather(up_keyval, "load", axis=0, tiled=True)
    ring = tensor_count
    chunk = tokens.shape[0]
    small_cols = keyval_cols + 2 * rank_share
    small_terms = jnp.zeros((ring, chunk, small_cols), jnp.float32)
    query_terms = jnp.zeros((ring, chunk, query_cols), jnp.float32)
    shift = [(i, (i + 1) % ring) for i in range(ring)]
    held = tokens
    for step in range(ring):
        following = lax.ppermute(held, "tensor", shift) if step < ring - 1 else None
        owner = (tensor_index - step) % ring
        block_ids = owner * chunk + jnp.arange(chunk, dtype=jnp.int32)
        _, _, block_hot = tenant_table(block_ids, adapter_rank, token_lengths, adapter_slot)
        small_block = jnp.concatenate(
            [
                product(held, weight_keyval),
                select_slot(product(held, down_query), block_hot),
                select_slot(product(held, down_keyval), block_hot),
            ],
            axis=1,
        )
        small_terms = lax.dynamic_update_slice_in_dim(small_terms, small_block[None], owner, 0)
        query_terms = lax.dynamic_update_slice_in_dim(
            query_terms, product(held, weight_query)[None], owner, 0
        )
        if following is not None:
            following, small_terms, query_terms = lax.optimization_barrier(
                (following, small_terms, query_terms)
            )
        held = following
    small_summed = lax.psum_scatter(
        small_terms.reshape(ring * chunk, -1), ("seq", "load"), scatter_dimension=0, tiled=True
    )
    query_summed = lax.psum_scatter(
        query_terms.reshape(ring * chunk, -1), ("seq", "load"), scatter_dimension=0, tiled=True
    )
    token_ids = block_index * block_rows + jnp.arange(block_rows, dtype=jnp.int32)
    own_rank, own_first, slot_hot = tenant_table(
        token_ids, adapter_rank, token_lengths, adapter_slot
    )
    position = token_ids - own_first
    first_rank = tensor_index * rank_share
    low_query = scale_ranks(
        small_summed[:, keyval_cols : keyval_cols + rank_share], own_rank, first_rank
    )
    low_keyval = scale_ranks(small_summed[:, keyval_cols + rank_share :], own_rank, first_rank)
    low_both = lax.all_gather(
        jnp.concatenate([low_query, low_keyval], axis=1), "tensor", axis=1
    )
    full_query = low_both[:, :, :rank_share].reshape(block_rows, -1)
    full_keyval = low_both[:, :, rank_share:].reshape(block_rows, -1)
    wide_query = widen_slots(full_query, slot_hot)
    wide_keyval = widen_slots(full_keyval, slot_hot)
    delta_keyval = product(wide_keyval, up_keyval_all)
    keyval = small_summed[:, :keyval_cols] + delta_keyval
    kv_first_col = tensor_index * keyval_cols
    is_key = kv_first_col + jnp.arange(keyval_cols, dtype=jnp.int32) < KV_HEADS * HEAD_DIM
    kv_local = jnp.where(
        is_key[None, :], rotate_pairs(keyval, position, kv_first_col), keyval
    ).astype(jnp.bfloat16)
    kv_all = lax.all_gather(kv_local, "tensor", axis=1, tiled=True)
    heads_here = query_cols // HEAD_DIM
    group_size = HEADS // KV_HEADS
    kv_here = max(heads_here // group_size, 1)
    per_kv = heads_here // kv_here
    kv_first = tensor_index * heads_here // group_size
    key_cols = KV_HEADS * HEAD_DIM
    key_heads = lax.dynamic_slice_in_dim(
        kv_all, kv_first * HEAD_DIM, kv_here * HEAD_DIM, 1
    ).reshape(block_rows, kv_here, HEAD_DIM)
    value_heads = lax.dynamic_slice_in_dim(
        kv_all, key_cols + kv_first * HEAD_DIM, kv_here * HEAD_DIM, 1
    ).reshape(block_rows, kv_here, HEAD_DIM)
    both_heads = lax.all_gather(
        jnp.concatenate([key_heads, value_heads], axis=1), ("seq", "load"), axis=0, tiled=True
    )
    piece_keys = both_heads[:, :kv_here]
    piece_values = both_heads[:, kv_here:]
    delta_query = lax.optimization_barrier(product(wide_query, up_query_all))
    query_rows = rotate_pairs(
        query_summed + delta_query, position, tensor_index * query_cols
    ).astype(jnp.bfloat16)
    grouped = query_rows.reshape(block_rows, kv_here, per_kv, HEAD_DIM)
    key_ids = jnp.arange(piece_keys.shape[0], dtype=jnp.int32)
    visible = (key_ids[None, :] >= own_first[:, None]) & (key_ids[None, :] <= token_ids[:, None])
    scores = jnp.einsum(
        "qghd,kgd->ghqk", grouped, piece_keys, preferred_element_type=jnp.float32
    ) / math.sqrt(HEAD_DIM)
    scores = jnp.where(visible, scores, -1e30)
    row_top = jnp.max(scores, axis=3)
    exp_scores = jnp.where(visible, jnp.exp(scores - row_top[..., None]), 0.0)
    row_total = jnp.sum(exp_scores, axis=3)
    accumulated = jnp.einsum(
        "ghqk,kgd->ghqd",
        exp_scores.astype(jnp.bfloat16),
        piece_values,
        preferred_element_type=jnp.float32,
    )
    context = (accumulated / row_total[..., None]).astype(jnp.bfloat16)
    context = jnp.transpose(context, (2, 0, 1, 3)).reshape(block_rows, query_cols)
    return (context, kv_local)


def solution(mesh):
    placed = (
        P(("groups", "tensor"), ("seq", "load")),
        P(("seq", "load"), "tensor"),
        P(("seq", "load"), "tensor"),
        P(("seq", "load"), ("groups", "tensor")),
        P(("seq", "load"), ("groups", "tensor")),
        P(("groups", "load"), "tensor"),
        P(("groups", "load"), "tensor"),
        P("groups"),
        P("groups"),
        P("groups"),
    )
    return jax.shard_map(
        shards,
        mesh=mesh,
        in_specs=placed,
        out_specs=(P(("groups", "seq", "load"), "tensor"), P(("groups", "seq", "load"), "tensor")),
        check_vma=False,
    )
```

```python
import math

import jax
import jax.numpy as jnp
from jax import lax
from jax.sharding import PartitionSpec as P

HEADS = 128
KV_HEADS = 8
HEAD_DIM = 128
TENANTS = 4


ROPE_BASE = 500000.0
ADAPTER_ALPHA = 8.0


def product(left, right):
    return jnp.dot(left, right, preferred_element_type=jnp.float32)


def rotate_pairs(values, position, first_col):
    pair_count = values.shape[1] // 2
    pair_col = first_col + 2 * jnp.arange(pair_count, dtype=jnp.int32)
    within = pair_col % HEAD_DIM // 2
    frequency = jnp.exp(-(2.0 * within.astype(jnp.float32) / HEAD_DIM) * math.log(ROPE_BASE))
    angles = position.astype(jnp.float32)[:, None] * frequency[None, :]
    pair_view = values.reshape(values.shape[0], pair_count, 2)
    even_part = pair_view[:, :, 0]
    odd_part = pair_view[:, :, 1]
    cosine = jnp.cos(angles)
    sine_angle = jnp.sin(angles)
    turned = jnp.stack(
        [even_part * cosine - odd_part * sine_angle, even_part * sine_angle + odd_part * cosine],
        axis=2,
    )
    return turned.reshape(values.shape)


def tenant_table(token_ids, adapter_rank, token_lengths, adapter_slot):
    segment_ends = jnp.cumsum(token_lengths)
    begins = segment_ends - token_lengths
    owned_rows = (token_ids[:, None] >= begins[None, :]) & (
        token_ids[:, None] < segment_ends[None, :]
    )
    zero_int = jnp.zeros((), jnp.int32)
    own_rank = jnp.sum(jnp.where(owned_rows, adapter_rank[None, :], zero_int), axis=1)
    own_slot = jnp.sum(jnp.where(owned_rows, adapter_slot[None, :], zero_int), axis=1)
    own_first = jnp.sum(jnp.where(owned_rows, begins[None, :], zero_int), axis=1)
    slot_hot = own_slot[:, None] == jnp.arange(TENANTS, dtype=jnp.int32)[None, :]
    return (own_rank, own_first, slot_hot)


def select_slot(down_values, slot_hot):
    shaped = down_values.reshape(down_values.shape[0], -1, TENANTS)
    return jnp.sum(jnp.where(slot_hot[:, None, :], shaped, 0.0), axis=2)


def scale_ranks(picked, own_rank, first_rank):
    rank_index = first_rank + jnp.arange(picked.shape[1], dtype=jnp.int32)
    keep_mask = rank_index[None, :] < own_rank[:, None]
    factor = ADAPTER_ALPHA / jnp.sqrt(own_rank.astype(jnp.float32))
    return jnp.where(keep_mask, picked * factor[:, None], 0.0).astype(jnp.bfloat16)


def widen_slots(low_values, slot_hot):
    wide_rows = jnp.where(
        slot_hot[:, None, :], low_values[:, :, None], jnp.zeros((), low_values.dtype)
    )
    return wide_rows.reshape(low_values.shape[0], -1)


def ring_reduce_scatter(blocks, axis):
    count = lax.axis_size(axis)
    me = lax.axis_index(axis)
    if count == 1:
        return blocks[0]
    shift = [(i, (i + 1) % count) for i in range(count)]

    def pick(step):
        return lax.dynamic_index_in_dim(blocks, (me - 1 - step) % count, 0, keepdims=False)

    total = pick(0)
    for step in range(1, count):
        total = lax.ppermute(total, axis, shift) + pick(step)
    return total


def shards(
    tokens,
    weight_query,
    weight_keyval,
    down_query,
    down_keyval,
    up_query,
    up_keyval,
    adapter_rank,
    token_lengths,
    adapter_slot,
):
    tensor_count = lax.axis_size("tensor")
    block_count = lax.axis_size(("seq", "load"))
    tensor_index = lax.axis_index("tensor")
    block_index = lax.axis_index(("seq", "load"))
    query_cols = weight_query.shape[1]
    keyval_cols = weight_keyval.shape[1]
    rank_share = down_query.shape[1] // TENANTS
    block_rows = tokens.shape[0] * tensor_count // block_count
    up_query_all = lax.all_gather(up_query, "load", axis=0, tiled=True)
    up_keyval_all = lax.all_gather(up_keyval, "load", axis=0, tiled=True)
    ring = tensor_count
    chunk = tokens.shape[0]
    small_cols = keyval_cols + 2 * rank_share
    small_terms = jnp.zeros((ring, chunk, small_cols), jnp.float32)
    query_terms = jnp.zeros((ring, chunk, query_cols), jnp.float32)
    shift = [(i, (i + 1) % ring) for i in range(ring)]
    held = tokens
    for step in range(ring):
        following = lax.ppermute(held, "tensor", shift) if step < ring - 1 else None
        owner = (tensor_index - step) % ring
        block_ids = owner * chunk + jnp.arange(chunk, dtype=jnp.int32)
        _, _, block_hot = tenant_table(block_ids, adapter_rank, token_lengths, adapter_slot)
        small_block = jnp.concatenate(
            [
                product(held, weight_keyval),
                select_slot(product(held, down_query), block_hot),
                select_slot(product(held, down_keyval), block_hot),
            ],
            axis=1,
        )
        small_terms = lax.dynamic_update_slice_in_dim(small_terms, small_block[None], owner, 0)
        query_terms = lax.dynamic_update_slice_in_dim(
            query_terms, product(held, weight_query)[None], owner, 0
        )
        if following is not None:
            following, small_terms, query_terms = lax.optimization_barrier(
                (following, small_terms, query_terms)
            )
        held = following
    seq_count = lax.axis_size("seq")
    load_count = lax.axis_size("load")
    by_core = small_terms.reshape(seq_count, load_count, block_rows, -1)
    per_core = ring_reduce_scatter(jnp.moveaxis(by_core, 1, 0), "load")
    small_summed = ring_reduce_scatter(per_core, "seq")
    query_summed = lax.psum_scatter(
        query_terms.reshape(ring * chunk, -1), ("seq", "load"), scatter_dimension=0, tiled=True
    )
    token_ids = block_index * block_rows + jnp.arange(block_rows, dtype=jnp.int32)
    own_rank, own_first, slot_hot = tenant_table(
        token_ids, adapter_rank, token_lengths, adapter_slot
    )
    position = token_ids - own_first
    first_rank = tensor_index * rank_share
    low_query = scale_ranks(
        small_summed[:, keyval_cols : keyval_cols + rank_share], own_rank, first_rank
    )
    low_keyval = scale_ranks(small_summed[:, keyval_cols + rank_share :], own_rank, first_rank)
    low_both = lax.all_gather(
        jnp.concatenate([low_query, low_keyval], axis=1), "tensor", axis=1
    )
    full_query = low_both[:, :, :rank_share].reshape(block_rows, -1)
    full_keyval = low_both[:, :, rank_share:].reshape(block_rows, -1)
    wide_query = widen_slots(full_query, slot_hot)
    wide_keyval = widen_slots(full_keyval, slot_hot)
    delta_keyval = product(wide_keyval, up_keyval_all)
    keyval = small_summed[:, :keyval_cols] + delta_keyval
    kv_first_col = tensor_index * keyval_cols
    is_key = kv_first_col + jnp.arange(keyval_cols, dtype=jnp.int32) < KV_HEADS * HEAD_DIM
    kv_local = jnp.where(
        is_key[None, :], rotate_pairs(keyval, position, kv_first_col), keyval
    ).astype(jnp.bfloat16)
    kv_all = lax.all_gather(kv_local, "tensor", axis=1, tiled=True)
    heads_here = query_cols // HEAD_DIM
    group_size = HEADS // KV_HEADS
    kv_here = max(heads_here // group_size, 1)
    per_kv = heads_here // kv_here
    kv_first = tensor_index * heads_here // group_size
    key_cols = KV_HEADS * HEAD_DIM
    key_heads = lax.dynamic_slice_in_dim(
        kv_all, kv_first * HEAD_DIM, kv_here * HEAD_DIM, 1
    ).reshape(block_rows, kv_here, HEAD_DIM)
    value_heads = lax.dynamic_slice_in_dim(
        kv_all, key_cols + kv_first * HEAD_DIM, kv_here * HEAD_DIM, 1
    ).reshape(block_rows, kv_here, HEAD_DIM)
    both_heads = lax.all_gather(
        jnp.concatenate([key_heads, value_heads], axis=1), ("seq", "load"), axis=0, tiled=True
    )
    piece_keys = both_heads[:, :kv_here]
    piece_values = both_heads[:, kv_here:]
    delta_query = lax.optimization_barrier(product(wide_query, up_query_all))
    query_rows = rotate_pairs(
        query_summed + delta_query, position, tensor_index * query_cols
    ).astype(jnp.bfloat16)
    grouped = query_rows.reshape(block_rows, kv_here, per_kv, HEAD_DIM)
    key_ids = jnp.arange(piece_keys.shape[0], dtype=jnp.int32)
    visible = (key_ids[None, :] >= own_first[:, None]) & (key_ids[None, :] <= token_ids[:, None])
    scores = jnp.einsum(
        "qghd,kgd->ghqk", grouped, piece_keys, preferred_element_type=jnp.float32
    ) / math.sqrt(HEAD_DIM)
    scores = jnp.where(visible, scores, -1e30)
    row_top = jnp.max(scores, axis=3)
    exp_scores = jnp.where(visible, jnp.exp(scores - row_top[..., None]), 0.0)
    row_total = jnp.sum(exp_scores, axis=3)
    accumulated = jnp.einsum(
        "ghqk,kgd->ghqd",
        exp_scores.astype(jnp.bfloat16),
        piece_values,
        preferred_element_type=jnp.float32,
    )
    context = (accumulated / row_total[..., None]).astype(jnp.bfloat16)
    context = jnp.transpose(context, (2, 0, 1, 3)).reshape(block_rows, query_cols)
    return (context, kv_local)


def solution(mesh):
    placed = (
        P(("groups", "tensor"), ("seq", "load")),
        P(("seq", "load"), "tensor"),
        P(("seq", "load"), "tensor"),
        P(("seq", "load"), ("groups", "tensor")),
        P(("seq", "load"), ("groups", "tensor")),
        P(("groups", "load"), "tensor"),
        P(("groups", "load"), "tensor"),
        P("groups"),
        P("groups"),
        P("groups"),
    )
    return jax.shard_map(
        shards,
        mesh=mesh,
        in_specs=placed,
        out_specs=(P(("groups", "seq", "load"), "tensor"), P(("groups", "seq", "load"), "tensor")),
        check_vma=False,
    )
```

```python
import math

import jax
import jax.numpy as jnp
from jax import lax
from jax.sharding import PartitionSpec as P

HEADS = 128
KV_HEADS = 8
HEAD_DIM = 128
TENANTS = 4


ROPE_BASE = 500000.0
ADAPTER_ALPHA = 8.0


def product(left, right):
    return jnp.dot(left, right, preferred_element_type=jnp.float32)


def rotate_pairs(values, position, first_col):
    cols = values.shape[1]
    width = HEAD_DIM if cols % HEAD_DIM == 0 else cols
    col = jnp.arange(width, dtype=jnp.int32)
    pair_col = first_col + col - col % 2
    within = pair_col % HEAD_DIM // 2
    frequency = jnp.exp(-(2.0 * within.astype(jnp.float32) / HEAD_DIM) * math.log(ROPE_BASE))
    angles = position.astype(jnp.float32)[:, None] * frequency[None, :]
    cosine = jnp.cos(angles)
    sine_angle = jnp.sin(angles)
    signed_sine = jnp.where((col % 2 == 0)[None, :], -sine_angle, sine_angle)
    cosine = jnp.tile(cosine, (1, cols // width))
    signed_sine = jnp.tile(signed_sine, (1, cols // width))
    is_even = (jnp.arange(cols, dtype=jnp.int32) % 2 == 0)[None, :]
    partner = jnp.where(is_even, jnp.roll(values, -1, axis=1), jnp.roll(values, 1, axis=1))
    return values * cosine + partner * signed_sine


def tenant_table(token_ids, adapter_rank, token_lengths, adapter_slot):
    segment_ends = jnp.cumsum(token_lengths)
    begins = segment_ends - token_lengths
    owned_rows = (token_ids[:, None] >= begins[None, :]) & (
        token_ids[:, None] < segment_ends[None, :]
    )
    zero_int = jnp.zeros((), jnp.int32)
    own_rank = jnp.sum(jnp.where(owned_rows, adapter_rank[None, :], zero_int), axis=1)
    own_slot = jnp.sum(jnp.where(owned_rows, adapter_slot[None, :], zero_int), axis=1)
    own_first = jnp.sum(jnp.where(owned_rows, begins[None, :], zero_int), axis=1)
    slot_hot = own_slot[:, None] == jnp.arange(TENANTS, dtype=jnp.int32)[None, :]
    return (own_rank, own_first, slot_hot)


def select_slot(down_values, slot_hot):
    shaped = down_values.reshape(down_values.shape[0], -1, TENANTS)
    return jnp.sum(jnp.where(slot_hot[:, None, :], shaped, 0.0), axis=2)


def scale_ranks(picked, own_rank, first_rank):
    rank_index = first_rank + jnp.arange(picked.shape[1], dtype=jnp.int32)
    keep_mask = rank_index[None, :] < own_rank[:, None]
    factor = ADAPTER_ALPHA / jnp.sqrt(own_rank.astype(jnp.float32))
    return jnp.where(keep_mask, picked * factor[:, None], 0.0).astype(jnp.bfloat16)


def widen_slots(low_values, slot_hot):
    wide_rows = jnp.where(
        slot_hot[:, None, :], low_values[:, :, None], jnp.zeros((), low_values.dtype)
    )
    return wide_rows.reshape(low_values.shape[0], -1)


def ring_reduce_scatter(blocks, axis):
    count = lax.axis_size(axis)
    me = lax.axis_index(axis)
    if count == 1:
        return blocks[0]
    shift = [(i, (i + 1) % count) for i in range(count)]

    def pick(step):
        return lax.dynamic_index_in_dim(blocks, (me - 1 - step) % count, 0, keepdims=False)

    total = pick(0)
    for step in range(1, count):
        total = lax.ppermute(total, axis, shift) + pick(step)
    return total


def shards(
    tokens,
    weight_query,
    weight_keyval,
    down_query,
    down_keyval,
    up_query,
    up_keyval,
    adapter_rank,
    token_lengths,
    adapter_slot,
):
    tensor_count = lax.axis_size("tensor")
    block_count = lax.axis_size(("seq", "load"))
    tensor_index = lax.axis_index("tensor")
    block_index = lax.axis_index(("seq", "load"))
    query_cols = weight_query.shape[1]
    keyval_cols = weight_keyval.shape[1]
    rank_share = down_query.shape[1] // TENANTS
    block_rows = tokens.shape[0] * tensor_count // block_count
    up_query_all = lax.all_gather(up_query, "load", axis=0, tiled=True)
    up_keyval_all = lax.all_gather(up_keyval, "load", axis=0, tiled=True)
    ring = tensor_count
    chunk = tokens.shape[0]
    small_cols = keyval_cols + 2 * rank_share
    small_terms = jnp.zeros((ring, chunk, small_cols), jnp.float32)
    query_terms = jnp.zeros((ring, chunk, query_cols), jnp.float32)
    shift = [(i, (i + 1) % ring) for i in range(ring)]
    held = tokens
    for step in range(ring):
        following = lax.ppermute(held, "tensor", shift) if step < ring - 1 else None
        owner = (tensor_index - step) % ring
        block_ids = owner * chunk + jnp.arange(chunk, dtype=jnp.int32)
        _, _, block_hot = tenant_table(block_ids, adapter_rank, token_lengths, adapter_slot)
        small_block = jnp.concatenate(
            [
                product(held, weight_keyval),
                select_slot(product(held, down_query), block_hot),
                select_slot(product(held, down_keyval), block_hot),
            ],
            axis=1,
        )
        small_terms = lax.dynamic_update_slice_in_dim(small_terms, small_block[None], owner, 0)
        query_terms = lax.dynamic_update_slice_in_dim(
            query_terms, product(held, weight_query)[None], owner, 0
        )
        if following is not None:
            following, small_terms, query_terms = lax.optimization_barrier(
                (following, small_terms, query_terms)
            )
        held = following
    seq_count = lax.axis_size("seq")
    load_count = lax.axis_size("load")
    by_core = small_terms.reshape(seq_count, load_count, block_rows, -1)
    per_core = ring_reduce_scatter(jnp.moveaxis(by_core, 1, 0), "load")
    small_summed = ring_reduce_scatter(per_core, "seq")
    query_summed = lax.psum_scatter(
        query_terms.reshape(ring * chunk, -1), ("seq", "load"), scatter_dimension=0, tiled=True
    )
    token_ids = block_index * block_rows + jnp.arange(block_rows, dtype=jnp.int32)
    own_rank, own_first, slot_hot = tenant_table(
        token_ids, adapter_rank, token_lengths, adapter_slot
    )
    position = token_ids - own_first
    first_rank = tensor_index * rank_share
    low_query = scale_ranks(
        small_summed[:, keyval_cols : keyval_cols + rank_share], own_rank, first_rank
    )
    low_keyval = scale_ranks(small_summed[:, keyval_cols + rank_share :], own_rank, first_rank)
    low_both = lax.all_gather(
        jnp.concatenate([low_query, low_keyval], axis=1), "tensor", axis=1
    )
    full_query = low_both[:, :, :rank_share].reshape(block_rows, -1)
    full_keyval = low_both[:, :, rank_share:].reshape(block_rows, -1)
    wide_query = widen_slots(full_query, slot_hot)
    wide_keyval = widen_slots(full_keyval, slot_hot)
    delta_keyval = product(wide_keyval, up_keyval_all)
    keyval = small_summed[:, :keyval_cols] + delta_keyval
    kv_first_col = tensor_index * keyval_cols
    is_key = kv_first_col + jnp.arange(keyval_cols, dtype=jnp.int32) < KV_HEADS * HEAD_DIM
    kv_local = jnp.where(
        is_key[None, :], rotate_pairs(keyval, position, kv_first_col), keyval
    ).astype(jnp.bfloat16)
    kv_all = lax.all_gather(kv_local, "tensor", axis=1, tiled=True)
    heads_here = query_cols // HEAD_DIM
    group_size = HEADS // KV_HEADS
    kv_here = max(heads_here // group_size, 1)
    per_kv = heads_here // kv_here
    kv_first = tensor_index * heads_here // group_size
    key_cols = KV_HEADS * HEAD_DIM
    key_heads = lax.dynamic_slice_in_dim(
        kv_all, kv_first * HEAD_DIM, kv_here * HEAD_DIM, 1
    ).reshape(block_rows, kv_here, HEAD_DIM)
    value_heads = lax.dynamic_slice_in_dim(
        kv_all, key_cols + kv_first * HEAD_DIM, kv_here * HEAD_DIM, 1
    ).reshape(block_rows, kv_here, HEAD_DIM)
    both_heads = lax.all_gather(
        jnp.concatenate([key_heads, value_heads], axis=1), ("seq", "load"), axis=0, tiled=True
    )
    piece_keys = both_heads[:, :kv_here]
    piece_values = both_heads[:, kv_here:]
    delta_query = lax.optimization_barrier(product(wide_query, up_query_all))
    query_rows = rotate_pairs(
        query_summed + delta_query, position, tensor_index * query_cols
    ).astype(jnp.bfloat16)
    grouped = query_rows.reshape(block_rows, kv_here, per_kv, HEAD_DIM)
    key_ids = jnp.arange(piece_keys.shape[0], dtype=jnp.int32)
    visible = (key_ids[None, :] >= own_first[:, None]) & (key_ids[None, :] <= token_ids[:, None])
    scores = jnp.einsum(
        "qghd,kgd->ghqk", grouped, piece_keys, preferred_element_type=jnp.float32
    ) / math.sqrt(HEAD_DIM)
    scores = jnp.where(visible, scores, -1e30)
    row_top = jnp.max(scores, axis=3)
    exp_scores = jnp.where(visible, jnp.exp(scores - row_top[..., None]), 0.0)
    row_total = jnp.sum(exp_scores, axis=3)
    accumulated = jnp.einsum(
        "ghqk,kgd->ghqd",
        exp_scores.astype(jnp.bfloat16),
        piece_values,
        preferred_element_type=jnp.float32,
    )
    context = (accumulated / row_total[..., None]).astype(jnp.bfloat16)
    context = jnp.transpose(context, (2, 0, 1, 3)).reshape(block_rows, query_cols)
    return (context, kv_local)


def solution(mesh):
    placed = (
        P(("groups", "tensor"), ("seq", "load")),
        P(("seq", "load"), "tensor"),
        P(("seq", "load"), "tensor"),
        P(("seq", "load"), ("groups", "tensor")),
        P(("seq", "load"), ("groups", "tensor")),
        P(("groups", "load"), "tensor"),
        P(("groups", "load"), "tensor"),
        P("groups"),
        P("groups"),
        P("groups"),
    )
    return jax.shard_map(
        shards,
        mesh=mesh,
        in_specs=placed,
        out_specs=(P(("groups", "seq", "load"), "tensor"), P(("groups", "seq", "load"), "tensor")),
        check_vma=False,
    )
```

```python
import math

import jax
import jax.numpy as jnp
from jax import lax
from jax.sharding import PartitionSpec as P

HEADS = 128
KV_HEADS = 8
HEAD_DIM = 128
TENANTS = 4


ROPE_BASE = 500000.0
ADAPTER_ALPHA = 8.0


def product(left, right):
    return jnp.dot(left, right, preferred_element_type=jnp.float32)


def rotate_pairs(values, position, first_col):
    cols = values.shape[1]
    width = HEAD_DIM if cols % HEAD_DIM == 0 else cols
    col = jnp.arange(width, dtype=jnp.int32)
    pair_col = first_col + col - col % 2
    within = pair_col % HEAD_DIM // 2
    frequency = jnp.exp(-(2.0 * within.astype(jnp.float32) / HEAD_DIM) * math.log(ROPE_BASE))
    angles = position.astype(jnp.float32)[:, None] * frequency[None, :]
    cosine = jnp.cos(angles)
    sine_angle = jnp.sin(angles)
    signed_sine = jnp.where((col % 2 == 0)[None, :], -sine_angle, sine_angle)
    cosine = jnp.tile(cosine, (1, cols // width))
    signed_sine = jnp.tile(signed_sine, (1, cols // width))
    is_even = (jnp.arange(cols, dtype=jnp.int32) % 2 == 0)[None, :]
    partner = jnp.where(is_even, jnp.roll(values, -1, axis=1), jnp.roll(values, 1, axis=1))
    return values * cosine + partner * signed_sine


def tenant_table(token_ids, adapter_rank, token_lengths, adapter_slot):
    segment_ends = jnp.cumsum(token_lengths)
    begins = segment_ends - token_lengths
    owned_rows = (token_ids[:, None] >= begins[None, :]) & (
        token_ids[:, None] < segment_ends[None, :]
    )
    zero_int = jnp.zeros((), jnp.int32)
    own_rank = jnp.sum(jnp.where(owned_rows, adapter_rank[None, :], zero_int), axis=1)
    own_slot = jnp.sum(jnp.where(owned_rows, adapter_slot[None, :], zero_int), axis=1)
    own_first = jnp.sum(jnp.where(owned_rows, begins[None, :], zero_int), axis=1)
    slot_hot = own_slot[:, None] == jnp.arange(TENANTS, dtype=jnp.int32)[None, :]
    return (own_rank, own_first, slot_hot)


def select_slot(down_values, slot_hot):
    shaped = down_values.reshape(down_values.shape[0], -1, TENANTS)
    return jnp.sum(jnp.where(slot_hot[:, None, :], shaped, 0.0), axis=2)


def scale_ranks(picked, own_rank, first_rank):
    rank_index = first_rank + jnp.arange(picked.shape[1], dtype=jnp.int32)
    keep_mask = rank_index[None, :] < own_rank[:, None]
    factor = ADAPTER_ALPHA / jnp.sqrt(own_rank.astype(jnp.float32))
    return jnp.where(keep_mask, picked * factor[:, None], 0.0).astype(jnp.bfloat16)


def widen_slots(low_values, slot_hot):
    wide_rows = jnp.where(
        slot_hot[:, None, :], low_values[:, :, None], jnp.zeros((), low_values.dtype)
    )
    return wide_rows.reshape(low_values.shape[0], -1)


def ring_reduce_scatter(blocks, axis):
    count = lax.axis_size(axis)
    me = lax.axis_index(axis)
    if count == 1:
        return blocks[0]
    shift = [(i, (i + 1) % count) for i in range(count)]

    def pick(step):
        return lax.dynamic_index_in_dim(blocks, (me - 1 - step) % count, 0, keepdims=False)

    total = pick(0)
    for step in range(1, count):
        total = lax.ppermute(total, axis, shift) + pick(step)
    return total


def shards(
    tokens,
    weight_query,
    weight_keyval,
    down_query,
    down_keyval,
    up_query,
    up_keyval,
    adapter_rank,
    token_lengths,
    adapter_slot,
):
    tensor_count = lax.axis_size("tensor")
    block_count = lax.axis_size(("seq", "load"))
    tensor_index = lax.axis_index("tensor")
    block_index = lax.axis_index(("seq", "load"))
    query_cols = weight_query.shape[1]
    keyval_cols = weight_keyval.shape[1]
    rank_share = down_query.shape[1] // TENANTS
    block_rows = tokens.shape[0] * tensor_count // block_count
    up_query_all = lax.all_gather(up_query, "load", axis=0, tiled=True)
    up_keyval_all = lax.all_gather(up_keyval, "load", axis=0, tiled=True)
    ring = tensor_count
    chunk = tokens.shape[0]
    seq_count = lax.axis_size("seq")
    load_count = lax.axis_size("load")
    load_index = lax.axis_index("load")
    small_cols = keyval_cols + 2 * rank_share
    small_terms = jnp.zeros((ring, chunk, small_cols), jnp.float32)
    kept_rows = seq_count * block_rows
    query_terms = jnp.zeros((kept_rows + chunk, query_cols), jnp.float32)
    core_swap = [(i, (i + 1) % load_count) for i in range(load_count)]
    shift = [(i, (i + 1) % ring) for i in range(ring)]
    held = tokens
    for step in range(ring):
        following = lax.ppermute(held, "tensor", shift) if step < ring - 1 else None
        owner = (tensor_index - step) % ring
        block_ids = owner * chunk + jnp.arange(chunk, dtype=jnp.int32)
        _, _, block_hot = tenant_table(block_ids, adapter_rank, token_lengths, adapter_slot)
        small_block = jnp.concatenate(
            [
                product(held, weight_keyval),
                select_slot(product(held, down_query), block_hot),
                select_slot(product(held, down_keyval), block_hot),
            ],
            axis=1,
        )
        small_terms = lax.dynamic_update_slice_in_dim(small_terms, small_block[None], owner, 0)
        query_block = product(held, weight_query)
        if load_count > 1:
            query_block = query_block + lax.ppermute(query_block, "load", core_swap)
        out_block = owner * chunk // block_rows
        keeps = out_block % load_count == load_index
        row_at = (out_block // load_count) * block_rows + owner * chunk % block_rows
        query_terms = lax.dynamic_update_slice_in_dim(
            query_terms, query_block, jnp.where(keeps, row_at, kept_rows), 0
        )
        if following is not None:
            following, small_terms, query_terms = lax.optimization_barrier(
                (following, small_terms, query_terms)
            )
        held = following
    by_core = small_terms.reshape(seq_count, load_count, block_rows, -1)
    per_core = ring_reduce_scatter(jnp.moveaxis(by_core, 1, 0), "load")
    small_summed = ring_reduce_scatter(per_core, "seq")
    query_summed = lax.psum_scatter(
        query_terms[:kept_rows], "seq", scatter_dimension=0, tiled=True
    )
    token_ids = block_index * block_rows + jnp.arange(block_rows, dtype=jnp.int32)
    own_rank, own_first, slot_hot = tenant_table(
        token_ids, adapter_rank, token_lengths, adapter_slot
    )
    position = token_ids - own_first
    first_rank = tensor_index * rank_share
    low_query = scale_ranks(
        small_summed[:, keyval_cols : keyval_cols + rank_share], own_rank, first_rank
    )
    low_keyval = scale_ranks(small_summed[:, keyval_cols + rank_share :], own_rank, first_rank)
    low_both = lax.all_gather(
        jnp.concatenate([low_query, low_keyval], axis=1), "tensor", axis=1
    )
    full_query = low_both[:, :, :rank_share].reshape(block_rows, -1)
    full_keyval = low_both[:, :, rank_share:].reshape(block_rows, -1)
    wide_query = widen_slots(full_query, slot_hot)
    wide_keyval = widen_slots(full_keyval, slot_hot)
    delta_keyval = product(wide_keyval, up_keyval_all)
    keyval = small_summed[:, :keyval_cols] + delta_keyval
    kv_first_col = tensor_index * keyval_cols
    is_key = kv_first_col + jnp.arange(keyval_cols, dtype=jnp.int32) < KV_HEADS * HEAD_DIM
    kv_local = jnp.where(
        is_key[None, :], rotate_pairs(keyval, position, kv_first_col), keyval
    ).astype(jnp.bfloat16)
    kv_all = lax.all_gather(kv_local, "tensor", axis=1, tiled=True)
    heads_here = query_cols // HEAD_DIM
    group_size = HEADS // KV_HEADS
    kv_here = max(heads_here // group_size, 1)
    per_kv = heads_here // kv_here
    kv_first = tensor_index * heads_here // group_size
    key_cols = KV_HEADS * HEAD_DIM
    key_heads = lax.dynamic_slice_in_dim(
        kv_all, kv_first * HEAD_DIM, kv_here * HEAD_DIM, 1
    ).reshape(block_rows, kv_here, HEAD_DIM)
    value_heads = lax.dynamic_slice_in_dim(
        kv_all, key_cols + kv_first * HEAD_DIM, kv_here * HEAD_DIM, 1
    ).reshape(block_rows, kv_here, HEAD_DIM)
    both_heads = lax.all_gather(
        jnp.concatenate([key_heads, value_heads], axis=1), ("seq", "load"), axis=0, tiled=True
    )
    piece_keys = both_heads[:, :kv_here]
    piece_values = both_heads[:, kv_here:]
    delta_query = lax.optimization_barrier(product(wide_query, up_query_all))
    query_rows = rotate_pairs(
        query_summed + delta_query, position, tensor_index * query_cols
    ).astype(jnp.bfloat16)
    grouped = query_rows.reshape(block_rows, kv_here, per_kv, HEAD_DIM)
    key_ids = jnp.arange(piece_keys.shape[0], dtype=jnp.int32)
    visible = (key_ids[None, :] >= own_first[:, None]) & (key_ids[None, :] <= token_ids[:, None])
    scores = jnp.einsum(
        "qghd,kgd->ghqk", grouped, piece_keys, preferred_element_type=jnp.float32
    ) / math.sqrt(HEAD_DIM)
    scores = jnp.where(visible, scores, -1e30)
    row_top = jnp.max(scores, axis=3)
    exp_scores = jnp.where(visible, jnp.exp(scores - row_top[..., None]), 0.0)
    row_total = jnp.sum(exp_scores, axis=3)
    accumulated = jnp.einsum(
        "ghqk,kgd->ghqd",
        exp_scores.astype(jnp.bfloat16),
        piece_values,
        preferred_element_type=jnp.float32,
    )
    context = (accumulated / row_total[..., None]).astype(jnp.bfloat16)
    context = jnp.transpose(context, (2, 0, 1, 3)).reshape(block_rows, query_cols)
    return (context, kv_local)


def solution(mesh):
    placed = (
        P(("groups", "tensor"), ("seq", "load")),
        P(("seq", "load"), "tensor"),
        P(("seq", "load"), "tensor"),
        P(("seq", "load"), ("groups", "tensor")),
        P(("seq", "load"), ("groups", "tensor")),
        P(("groups", "load"), "tensor"),
        P(("groups", "load"), "tensor"),
        P("groups"),
        P("groups"),
        P("groups"),
    )
    return jax.shard_map(
        shards,
        mesh=mesh,
        in_specs=placed,
        out_specs=(P(("groups", "seq", "load"), "tensor"), P(("groups", "seq", "load"), "tensor")),
        check_vma=False,
    )
```

```python
import math

import jax
import jax.numpy as jnp
from jax import lax
from jax.sharding import PartitionSpec as P

HEADS = 128
KV_HEADS = 8
HEAD_DIM = 128
TENANTS = 4


ROPE_BASE = 500000.0
ADAPTER_ALPHA = 8.0


def product(left, right):
    return jnp.dot(left, right, preferred_element_type=jnp.float32)


def rotate_pairs(values, position, first_col):
    cols = values.shape[1]
    width = HEAD_DIM if cols % HEAD_DIM == 0 else cols
    col = jnp.arange(width, dtype=jnp.int32)
    pair_col = first_col + col - col % 2
    within = pair_col % HEAD_DIM // 2
    frequency = jnp.exp(-(2.0 * within.astype(jnp.float32) / HEAD_DIM) * math.log(ROPE_BASE))
    angles = position.astype(jnp.float32)[:, None] * frequency[None, :]
    cosine = jnp.cos(angles)
    sine_angle = jnp.sin(angles)
    signed_sine = jnp.where((col % 2 == 0)[None, :], -sine_angle, sine_angle)
    cosine = jnp.tile(cosine, (1, cols // width))
    signed_sine = jnp.tile(signed_sine, (1, cols // width))
    is_even = (jnp.arange(cols, dtype=jnp.int32) % 2 == 0)[None, :]
    partner = jnp.where(is_even, jnp.roll(values, -1, axis=1), jnp.roll(values, 1, axis=1))
    return values * cosine + partner * signed_sine


def tenant_table(token_ids, adapter_rank, token_lengths, adapter_slot):
    segment_ends = jnp.cumsum(token_lengths)
    begins = segment_ends - token_lengths
    owned_rows = (token_ids[:, None] >= begins[None, :]) & (
        token_ids[:, None] < segment_ends[None, :]
    )
    zero_int = jnp.zeros((), jnp.int32)
    own_rank = jnp.sum(jnp.where(owned_rows, adapter_rank[None, :], zero_int), axis=1)
    own_slot = jnp.sum(jnp.where(owned_rows, adapter_slot[None, :], zero_int), axis=1)
    own_first = jnp.sum(jnp.where(owned_rows, begins[None, :], zero_int), axis=1)
    slot_hot = own_slot[:, None] == jnp.arange(TENANTS, dtype=jnp.int32)[None, :]
    return (own_rank, own_first, slot_hot)


def select_slot(down_values, slot_hot):
    shaped = down_values.reshape(down_values.shape[0], -1, TENANTS)
    return jnp.sum(jnp.where(slot_hot[:, None, :], shaped, 0.0), axis=2)


def scale_ranks(picked, own_rank, first_rank):
    rank_index = first_rank + jnp.arange(picked.shape[1], dtype=jnp.int32)
    keep_mask = rank_index[None, :] < own_rank[:, None]
    factor = ADAPTER_ALPHA / jnp.sqrt(own_rank.astype(jnp.float32))
    return jnp.where(keep_mask, picked * factor[:, None], 0.0).astype(jnp.bfloat16)


def widen_slots(low_values, slot_hot):
    wide_rows = jnp.where(
        slot_hot[:, None, :], low_values[:, :, None], jnp.zeros((), low_values.dtype)
    )
    return wide_rows.reshape(low_values.shape[0], -1)


def ring_reduce_scatter(blocks, axis):
    count = lax.axis_size(axis)
    me = lax.axis_index(axis)
    if count == 1:
        return blocks[0]
    shift = [(i, (i + 1) % count) for i in range(count)]

    def pick(step):
        return lax.dynamic_index_in_dim(blocks, (me - 1 - step) % count, 0, keepdims=False)

    total = pick(0)
    for step in range(1, count):
        total = lax.ppermute(total, axis, shift) + pick(step)
    return total


def shards(
    tokens,
    weight_query,
    weight_keyval,
    down_query,
    down_keyval,
    up_query,
    up_keyval,
    adapter_rank,
    token_lengths,
    adapter_slot,
):
    tensor_count = lax.axis_size("tensor")
    block_count = lax.axis_size(("seq", "load"))
    tensor_index = lax.axis_index("tensor")
    block_index = lax.axis_index(("seq", "load"))
    query_cols = weight_query.shape[1]
    keyval_cols = weight_keyval.shape[1]
    rank_share = down_query.shape[1] // TENANTS
    block_rows = tokens.shape[0] * tensor_count // block_count
    up_query_all = lax.all_gather(up_query, "load", axis=0, tiled=True)
    up_keyval_all = lax.all_gather(up_keyval, "load", axis=0, tiled=True)
    ring = tensor_count
    chunk = tokens.shape[0]
    small_cols = keyval_cols + 2 * rank_share
    small_terms = jnp.zeros((ring, chunk, small_cols), jnp.float32)
    query_terms = jnp.zeros((ring, chunk, query_cols), jnp.float32)
    shift = [(i, (i + 1) % ring) for i in range(ring)]
    held = tokens
    for step in range(ring):
        following = lax.ppermute(held, "tensor", shift) if step < ring - 1 else None
        owner = (tensor_index - step) % ring
        block_ids = owner * chunk + jnp.arange(chunk, dtype=jnp.int32)
        _, _, block_hot = tenant_table(block_ids, adapter_rank, token_lengths, adapter_slot)
        small_block = jnp.concatenate(
            [
                product(held, weight_keyval),
                select_slot(product(held, down_query), block_hot),
                select_slot(product(held, down_keyval), block_hot),
            ],
            axis=1,
        )
        small_terms = lax.dynamic_update_slice_in_dim(small_terms, small_block[None], owner, 0)
        if step == 0 and ring > 2:
            first_block, first_owner = held, owner
        elif step == 1 and ring > 2:
            pair = product(jnp.concatenate([first_block, held], axis=0), weight_query)
            query_terms = lax.dynamic_update_slice_in_dim(
                query_terms, pair[:chunk][None], first_owner, 0
            )
            query_terms = lax.dynamic_update_slice_in_dim(
                query_terms, pair[chunk:][None], owner, 0
            )
        else:
            query_terms = lax.dynamic_update_slice_in_dim(
                query_terms, product(held, weight_query)[None], owner, 0
            )
        if following is not None:
            if step == 0 and ring > 2:
                following, small_terms, first_block = lax.optimization_barrier(
                    (following, small_terms, first_block)
                )
            else:
                following, small_terms, query_terms = lax.optimization_barrier(
                    (following, small_terms, query_terms)
                )
        held = following
    seq_count = lax.axis_size("seq")
    load_count = lax.axis_size("load")
    by_core = small_terms.reshape(seq_count, load_count, block_rows, -1)
    per_core = ring_reduce_scatter(jnp.moveaxis(by_core, 1, 0), "load")
    small_summed = ring_reduce_scatter(per_core, "seq")
    query_summed = lax.psum_scatter(
        query_terms.reshape(ring * chunk, -1), ("seq", "load"), scatter_dimension=0, tiled=True
    )
    token_ids = block_index * block_rows + jnp.arange(block_rows, dtype=jnp.int32)
    own_rank, own_first, slot_hot = tenant_table(
        token_ids, adapter_rank, token_lengths, adapter_slot
    )
    position = token_ids - own_first
    first_rank = tensor_index * rank_share
    low_query = scale_ranks(
        small_summed[:, keyval_cols : keyval_cols + rank_share], own_rank, first_rank
    )
    low_keyval = scale_ranks(small_summed[:, keyval_cols + rank_share :], own_rank, first_rank)
    low_both = lax.all_gather(
        jnp.concatenate([low_query, low_keyval], axis=1), "tensor", axis=1
    )
    full_query = low_both[:, :, :rank_share].reshape(block_rows, -1)
    full_keyval = low_both[:, :, rank_share:].reshape(block_rows, -1)
    wide_query = widen_slots(full_query, slot_hot)
    wide_keyval = widen_slots(full_keyval, slot_hot)
    delta_keyval = product(wide_keyval, up_keyval_all)
    keyval = small_summed[:, :keyval_cols] + delta_keyval
    kv_first_col = tensor_index * keyval_cols
    is_key = kv_first_col + jnp.arange(keyval_cols, dtype=jnp.int32) < KV_HEADS * HEAD_DIM
    kv_local = jnp.where(
        is_key[None, :], rotate_pairs(keyval, position, kv_first_col), keyval
    ).astype(jnp.bfloat16)
    kv_all = lax.all_gather(kv_local, "tensor", axis=1, tiled=True)
    heads_here = query_cols // HEAD_DIM
    group_size = HEADS // KV_HEADS
    kv_here = max(heads_here // group_size, 1)
    per_kv = heads_here // kv_here
    kv_first = tensor_index * heads_here // group_size
    key_cols = KV_HEADS * HEAD_DIM
    key_heads = lax.dynamic_slice_in_dim(
        kv_all, kv_first * HEAD_DIM, kv_here * HEAD_DIM, 1
    ).reshape(block_rows, kv_here, HEAD_DIM)
    value_heads = lax.dynamic_slice_in_dim(
        kv_all, key_cols + kv_first * HEAD_DIM, kv_here * HEAD_DIM, 1
    ).reshape(block_rows, kv_here, HEAD_DIM)
    both_heads = lax.all_gather(
        jnp.concatenate([key_heads, value_heads], axis=1), ("seq", "load"), axis=0, tiled=True
    )
    piece_keys = both_heads[:, :kv_here]
    piece_values = both_heads[:, kv_here:]
    delta_query = lax.optimization_barrier(product(wide_query, up_query_all))
    query_rows = rotate_pairs(
        query_summed + delta_query, position, tensor_index * query_cols
    ).astype(jnp.bfloat16)
    grouped = query_rows.reshape(block_rows, kv_here, per_kv, HEAD_DIM)
    key_ids = jnp.arange(piece_keys.shape[0], dtype=jnp.int32)
    visible = (key_ids[None, :] >= own_first[:, None]) & (key_ids[None, :] <= token_ids[:, None])
    scores = jnp.einsum(
        "qghd,kgd->ghqk", grouped, piece_keys, preferred_element_type=jnp.float32
    ) / math.sqrt(HEAD_DIM)
    scores = jnp.where(visible, scores, -1e30)
    row_top = jnp.max(scores, axis=3)
    exp_scores = jnp.where(visible, jnp.exp(scores - row_top[..., None]), 0.0)
    row_total = jnp.sum(exp_scores, axis=3)
    accumulated = jnp.einsum(
        "ghqk,kgd->ghqd",
        exp_scores.astype(jnp.bfloat16),
        piece_values,
        preferred_element_type=jnp.float32,
    )
    context = (accumulated / row_total[..., None]).astype(jnp.bfloat16)
    context = jnp.transpose(context, (2, 0, 1, 3)).reshape(block_rows, query_cols)
    return (context, kv_local)


def solution(mesh):
    placed = (
        P(("groups", "tensor"), ("seq", "load")),
        P(("seq", "load"), "tensor"),
        P(("seq", "load"), "tensor"),
        P(("seq", "load"), ("groups", "tensor")),
        P(("seq", "load"), ("groups", "tensor")),
        P(("groups", "load"), "tensor"),
        P(("groups", "load"), "tensor"),
        P("groups"),
        P("groups"),
        P("groups"),
    )
    return jax.shard_map(
        shards,
        mesh=mesh,
        in_specs=placed,
        out_specs=(P(("groups", "seq", "load"), "tensor"), P(("groups", "seq", "load"), "tensor")),
        check_vma=False,
    )
```

```python
import math

import jax
import jax.numpy as jnp
from jax import lax
from jax.sharding import PartitionSpec as P

HEADS = 128
KV_HEADS = 8
HEAD_DIM = 128
TENANTS = 4


ROPE_BASE = 500000.0
ADAPTER_ALPHA = 8.0


def product(left, right):
    return jnp.dot(left, right, preferred_element_type=jnp.float32)


def rotate_pairs(values, position, first_col):
    cols = values.shape[1]
    width = HEAD_DIM if cols % HEAD_DIM == 0 else cols
    col = jnp.arange(width, dtype=jnp.int32)
    pair_col = first_col + col - col % 2
    within = pair_col % HEAD_DIM // 2
    frequency = jnp.exp(-(2.0 * within.astype(jnp.float32) / HEAD_DIM) * math.log(ROPE_BASE))
    angles = position.astype(jnp.float32)[:, None] * frequency[None, :]
    cosine = jnp.cos(angles)
    sine_angle = jnp.sin(angles)
    signed_sine = jnp.where((col % 2 == 0)[None, :], -sine_angle, sine_angle)
    cosine = jnp.tile(cosine, (1, cols // width))
    signed_sine = jnp.tile(signed_sine, (1, cols // width))
    is_even = (jnp.arange(cols, dtype=jnp.int32) % 2 == 0)[None, :]
    partner = jnp.where(is_even, jnp.roll(values, -1, axis=1), jnp.roll(values, 1, axis=1))
    return values * cosine + partner * signed_sine


def tenant_table(token_ids, adapter_rank, token_lengths, adapter_slot):
    segment_ends = jnp.cumsum(token_lengths)
    begins = segment_ends - token_lengths
    owned_rows = (token_ids[:, None] >= begins[None, :]) & (
        token_ids[:, None] < segment_ends[None, :]
    )
    zero_int = jnp.zeros((), jnp.int32)
    own_rank = jnp.sum(jnp.where(owned_rows, adapter_rank[None, :], zero_int), axis=1)
    own_slot = jnp.sum(jnp.where(owned_rows, adapter_slot[None, :], zero_int), axis=1)
    own_first = jnp.sum(jnp.where(owned_rows, begins[None, :], zero_int), axis=1)
    slot_hot = own_slot[:, None] == jnp.arange(TENANTS, dtype=jnp.int32)[None, :]
    return (own_rank, own_first, slot_hot)


def select_slot(down_values, slot_hot):
    shaped = down_values.reshape(down_values.shape[0], -1, TENANTS)
    return jnp.sum(jnp.where(slot_hot[:, None, :], shaped, 0.0), axis=2)


def scale_ranks(picked, own_rank, first_rank):
    rank_index = first_rank + jnp.arange(picked.shape[1], dtype=jnp.int32)
    keep_mask = rank_index[None, :] < own_rank[:, None]
    factor = ADAPTER_ALPHA / jnp.sqrt(own_rank.astype(jnp.float32))
    return jnp.where(keep_mask, picked * factor[:, None], 0.0).astype(jnp.bfloat16)


def widen_slots(low_values, slot_hot):
    wide_rows = jnp.where(
        slot_hot[:, None, :], low_values[:, :, None], jnp.zeros((), low_values.dtype)
    )
    return wide_rows.reshape(low_values.shape[0], -1)


def ring_reduce_scatter(blocks, axis):
    count = lax.axis_size(axis)
    me = lax.axis_index(axis)
    if count == 1:
        return blocks[0]
    shift = [(i, (i + 1) % count) for i in range(count)]

    def pick(step):
        return lax.dynamic_index_in_dim(blocks, (me - 1 - step) % count, 0, keepdims=False)

    total = pick(0)
    for step in range(1, count):
        total = lax.ppermute(total, axis, shift) + pick(step)
    return total


def shards(
    tokens,
    weight_query,
    weight_keyval,
    down_query,
    down_keyval,
    up_query,
    up_keyval,
    adapter_rank,
    token_lengths,
    adapter_slot,
):
    tensor_count = lax.axis_size("tensor")
    block_count = lax.axis_size(("seq", "load"))
    tensor_index = lax.axis_index("tensor")
    block_index = lax.axis_index(("seq", "load"))
    query_cols = weight_query.shape[1]
    keyval_cols = weight_keyval.shape[1]
    rank_share = down_query.shape[1] // TENANTS
    block_rows = tokens.shape[0] * tensor_count // block_count
    up_query_all = lax.all_gather(up_query, "load", axis=0, tiled=True)
    up_keyval_all = lax.all_gather(up_keyval, "load", axis=0, tiled=True)
    ring = tensor_count
    chunk = tokens.shape[0]
    small_cols = keyval_cols + 2 * rank_share
    small_terms = jnp.zeros((ring, chunk, small_cols), jnp.float32)
    query_terms = jnp.zeros((ring, chunk, query_cols), jnp.float32)
    shift = [(i, (i + 1) % ring) for i in range(ring)]
    held = tokens
    for step in range(ring):
        following = lax.ppermute(held, "tensor", shift) if step < ring - 1 else None
        owner = (tensor_index - step) % ring
        block_ids = owner * chunk + jnp.arange(chunk, dtype=jnp.int32)
        _, _, block_hot = tenant_table(block_ids, adapter_rank, token_lengths, adapter_slot)
        small_block = jnp.concatenate(
            [
                product(held, weight_keyval),
                select_slot(product(held, down_query), block_hot),
                select_slot(product(held, down_keyval), block_hot),
            ],
            axis=1,
        )
        small_terms = lax.dynamic_update_slice_in_dim(small_terms, small_block[None], owner, 0)
        if step == 0 and ring > 2:
            first_block, first_owner = held, owner
        elif step == 1 and ring > 2:
            pair = product(jnp.concatenate([first_block, held], axis=0), weight_query)
            query_terms = lax.dynamic_update_slice_in_dim(
                query_terms, pair[:chunk][None], first_owner, 0
            )
            query_terms = lax.dynamic_update_slice_in_dim(
                query_terms, pair[chunk:][None], owner, 0
            )
        else:
            query_terms = lax.dynamic_update_slice_in_dim(
                query_terms, product(held, weight_query)[None], owner, 0
            )
        if following is not None:
            if step == 0 and ring > 2:
                following, small_terms, first_block = lax.optimization_barrier(
                    (following, small_terms, first_block)
                )
            else:
                following, small_terms, query_terms = lax.optimization_barrier(
                    (following, small_terms, query_terms)
                )
        held = following
    seq_count = lax.axis_size("seq")
    load_count = lax.axis_size("load")
    by_core = small_terms.reshape(seq_count, load_count, block_rows, -1)
    per_core = ring_reduce_scatter(jnp.moveaxis(by_core, 1, 0), "load")
    small_summed = ring_reduce_scatter(per_core, "seq")
    query_summed = lax.psum_scatter(
        query_terms.reshape(ring * chunk, -1), ("seq", "load"), scatter_dimension=0, tiled=True
    )
    token_ids = block_index * block_rows + jnp.arange(block_rows, dtype=jnp.int32)
    own_rank, own_first, slot_hot = tenant_table(
        token_ids, adapter_rank, token_lengths, adapter_slot
    )
    position = token_ids - own_first
    first_rank = tensor_index * rank_share
    low_query = scale_ranks(
        small_summed[:, keyval_cols : keyval_cols + rank_share], own_rank, first_rank
    )
    low_keyval = scale_ranks(small_summed[:, keyval_cols + rank_share :], own_rank, first_rank)
    low_both = lax.all_gather(
        jnp.concatenate([low_query, low_keyval], axis=1), "tensor", axis=1
    )
    full_query = low_both[:, :, :rank_share].reshape(block_rows, -1)
    full_keyval = low_both[:, :, rank_share:].reshape(block_rows, -1)
    wide_query = widen_slots(full_query, slot_hot)
    wide_keyval = widen_slots(full_keyval, slot_hot)
    delta_keyval = product(wide_keyval, up_keyval_all)
    keyval = small_summed[:, :keyval_cols] + delta_keyval
    kv_first_col = tensor_index * keyval_cols
    is_key = kv_first_col + jnp.arange(keyval_cols, dtype=jnp.int32) < KV_HEADS * HEAD_DIM
    kv_local = jnp.where(
        is_key[None, :], rotate_pairs(keyval, position, kv_first_col), keyval
    ).astype(jnp.bfloat16)
    kv_all = lax.all_gather(kv_local, "tensor", axis=1, tiled=True)
    heads_here = query_cols // HEAD_DIM
    group_size = HEADS // KV_HEADS
    kv_here = max(heads_here // group_size, 1)
    per_kv = heads_here // kv_here
    kv_first = tensor_index * heads_here // group_size
    key_cols = KV_HEADS * HEAD_DIM
    key_heads = lax.dynamic_slice_in_dim(
        kv_all, kv_first * HEAD_DIM, kv_here * HEAD_DIM, 1
    ).reshape(block_rows, kv_here, HEAD_DIM)
    value_heads = lax.dynamic_slice_in_dim(
        kv_all, key_cols + kv_first * HEAD_DIM, kv_here * HEAD_DIM, 1
    ).reshape(block_rows, kv_here, HEAD_DIM)
    both_heads = lax.all_gather(
        jnp.concatenate([key_heads, value_heads], axis=1), ("seq", "load"), axis=0, tiled=True
    )
    piece_keys = both_heads[:, :kv_here]
    piece_values = both_heads[:, kv_here:]
    delta_query = lax.optimization_barrier(product(wide_query, up_query_all))
    query_rows = lax.optimization_barrier(
        rotate_pairs(query_summed + delta_query, position, tensor_index * query_cols).astype(
            jnp.bfloat16
        )
    )
    grouped = query_rows.reshape(block_rows, kv_here, per_kv, HEAD_DIM)
    key_ids = jnp.arange(piece_keys.shape[0], dtype=jnp.int32)
    visible = (key_ids[None, :] >= own_first[:, None]) & (key_ids[None, :] <= token_ids[:, None])
    scores = jnp.einsum(
        "qghd,kgd->ghqk", grouped, piece_keys, preferred_element_type=jnp.float32
    ) / math.sqrt(HEAD_DIM)
    scores = jnp.where(visible, scores, -1e30)
    row_top = jnp.max(scores, axis=3)
    exp_scores = jnp.where(visible, jnp.exp(scores - row_top[..., None]), 0.0)
    row_total = jnp.sum(exp_scores, axis=3)
    accumulated = jnp.einsum(
        "ghqk,kgd->ghqd",
        exp_scores.astype(jnp.bfloat16),
        piece_values,
        preferred_element_type=jnp.float32,
    )
    context = (accumulated / row_total[..., None]).astype(jnp.bfloat16)
    context = jnp.transpose(context, (2, 0, 1, 3)).reshape(block_rows, query_cols)
    return (context, kv_local)


def solution(mesh):
    placed = (
        P(("groups", "tensor"), ("seq", "load")),
        P(("seq", "load"), "tensor"),
        P(("seq", "load"), "tensor"),
        P(("seq", "load"), ("groups", "tensor")),
        P(("seq", "load"), ("groups", "tensor")),
        P(("groups", "load"), "tensor"),
        P(("groups", "load"), "tensor"),
        P("groups"),
        P("groups"),
        P("groups"),
    )
    return jax.shard_map(
        shards,
        mesh=mesh,
        in_specs=placed,
        out_specs=(P(("groups", "seq", "load"), "tensor"), P(("groups", "seq", "load"), "tensor")),
        check_vma=False,
    )
```

```python
import math

import jax
import jax.numpy as jnp
from jax import lax
from jax.sharding import PartitionSpec as P

HEADS = 128
KV_HEADS = 8
HEAD_DIM = 128
TENANTS = 4


ROPE_BASE = 500000.0
ADAPTER_ALPHA = 8.0


def product(left, right):
    return jnp.dot(left, right, preferred_element_type=jnp.float32)


def rotate_pairs(values, position, first_col):
    cols = values.shape[1]
    width = HEAD_DIM if cols % HEAD_DIM == 0 else cols
    col = jnp.arange(width, dtype=jnp.int32)
    pair_col = first_col + col - col % 2
    within = pair_col % HEAD_DIM // 2
    frequency = jnp.exp(-(2.0 * within.astype(jnp.float32) / HEAD_DIM) * math.log(ROPE_BASE))
    angles = position.astype(jnp.float32)[:, None] * frequency[None, :]
    cosine = jnp.cos(angles)
    sine_angle = jnp.sin(angles)
    signed_sine = jnp.where((col % 2 == 0)[None, :], -sine_angle, sine_angle)
    cosine = jnp.tile(cosine, (1, cols // width))
    signed_sine = jnp.tile(signed_sine, (1, cols // width))
    is_even = (jnp.arange(cols, dtype=jnp.int32) % 2 == 0)[None, :]
    partner = jnp.where(is_even, jnp.roll(values, -1, axis=1), jnp.roll(values, 1, axis=1))
    return values * cosine + partner * signed_sine


def tenant_table(token_ids, adapter_rank, token_lengths, adapter_slot):
    segment_ends = jnp.cumsum(token_lengths)
    begins = segment_ends - token_lengths
    owned_rows = (token_ids[:, None] >= begins[None, :]) & (
        token_ids[:, None] < segment_ends[None, :]
    )
    zero_int = jnp.zeros((), jnp.int32)
    own_rank = jnp.sum(jnp.where(owned_rows, adapter_rank[None, :], zero_int), axis=1)
    own_slot = jnp.sum(jnp.where(owned_rows, adapter_slot[None, :], zero_int), axis=1)
    own_first = jnp.sum(jnp.where(owned_rows, begins[None, :], zero_int), axis=1)
    slot_hot = own_slot[:, None] == jnp.arange(TENANTS, dtype=jnp.int32)[None, :]
    return (own_rank, own_first, slot_hot)


def select_slot(down_values, slot_hot):
    shaped = down_values.reshape(down_values.shape[0], -1, TENANTS)
    return jnp.sum(jnp.where(slot_hot[:, None, :], shaped, 0.0), axis=2)


def scale_ranks(picked, own_rank, first_rank):
    rank_index = first_rank + jnp.arange(picked.shape[1], dtype=jnp.int32)
    keep_mask = rank_index[None, :] < own_rank[:, None]
    factor = ADAPTER_ALPHA / jnp.sqrt(own_rank.astype(jnp.float32))
    return jnp.where(keep_mask, picked * factor[:, None], 0.0).astype(jnp.bfloat16)


def widen_slots(low_values, slot_hot):
    wide_rows = jnp.where(
        slot_hot[:, None, :], low_values[:, :, None], jnp.zeros((), low_values.dtype)
    )
    return wide_rows.reshape(low_values.shape[0], -1)


def ring_reduce_scatter(blocks, axis):
    count = lax.axis_size(axis)
    me = lax.axis_index(axis)
    if count == 1:
        return blocks[0]
    shift = [(i, (i + 1) % count) for i in range(count)]

    def pick(step):
        return lax.dynamic_index_in_dim(blocks, (me - 1 - step) % count, 0, keepdims=False)

    total = pick(0)
    for step in range(1, count):
        total = lax.ppermute(total, axis, shift) + pick(step)
    return total


def shards(
    tokens,
    weight_query,
    weight_keyval,
    down_query,
    down_keyval,
    up_query,
    up_keyval,
    adapter_rank,
    token_lengths,
    adapter_slot,
):
    tensor_count = lax.axis_size("tensor")
    block_count = lax.axis_size(("seq", "load"))
    tensor_index = lax.axis_index("tensor")
    block_index = lax.axis_index(("seq", "load"))
    query_cols = weight_query.shape[1]
    keyval_cols = weight_keyval.shape[1]
    rank_share = down_query.shape[1] // TENANTS
    block_rows = tokens.shape[0] * tensor_count // block_count
    up_query_all = lax.all_gather(up_query, "load", axis=0, tiled=True)
    up_keyval_all = lax.all_gather(up_keyval, "load", axis=0, tiled=True)
    ring = tensor_count
    chunk = tokens.shape[0]
    small_cols = keyval_cols + 2 * rank_share
    small_terms = jnp.zeros((ring, chunk, small_cols), jnp.float32)
    query_terms = jnp.zeros((ring, chunk, query_cols), jnp.float32)
    seq_count = lax.axis_size("seq")
    load_count = lax.axis_size("load")
    rows_per_out = block_rows // chunk

    def query_slot(owner):
        out_block = owner // rows_per_out
        target = (out_block % load_count) * seq_count + out_block // load_count
        return target * rows_per_out + owner % rows_per_out

    shift = [(i, (i + 1) % ring) for i in range(ring)]
    held = tokens
    for step in range(ring):
        following = lax.ppermute(held, "tensor", shift) if step < ring - 1 else None
        owner = (tensor_index - step) % ring
        block_ids = owner * chunk + jnp.arange(chunk, dtype=jnp.int32)
        _, _, block_hot = tenant_table(block_ids, adapter_rank, token_lengths, adapter_slot)
        small_block = jnp.concatenate(
            [
                product(held, weight_keyval),
                select_slot(product(held, down_query), block_hot),
                select_slot(product(held, down_keyval), block_hot),
            ],
            axis=1,
        )
        small_terms = lax.dynamic_update_slice_in_dim(small_terms, small_block[None], owner, 0)
        if step == 0 and ring > 2:
            first_block, first_owner = held, owner
        elif step == 1 and ring > 2:
            pair = product(jnp.concatenate([first_block, held], axis=0), weight_query)
            query_terms = lax.dynamic_update_slice_in_dim(
                query_terms, pair[:chunk][None], query_slot(first_owner), 0
            )
            query_terms = lax.dynamic_update_slice_in_dim(
                query_terms, pair[chunk:][None], query_slot(owner), 0
            )
        else:
            query_terms = lax.dynamic_update_slice_in_dim(
                query_terms, product(held, weight_query)[None], query_slot(owner), 0
            )
        if following is not None:
            if step == 0 and ring > 2:
                following, small_terms, first_block = lax.optimization_barrier(
                    (following, small_terms, first_block)
                )
            else:
                following, small_terms, query_terms = lax.optimization_barrier(
                    (following, small_terms, query_terms)
                )
        held = following
    by_core = small_terms.reshape(seq_count, load_count, block_rows, -1)
    per_core = ring_reduce_scatter(jnp.moveaxis(by_core, 1, 0), "load")
    small_summed = ring_reduce_scatter(per_core, "seq")
    query_summed = lax.psum_scatter(
        query_terms.reshape(ring * chunk, -1), ("load", "seq"), scatter_dimension=0, tiled=True
    )
    token_ids = block_index * block_rows + jnp.arange(block_rows, dtype=jnp.int32)
    own_rank, own_first, slot_hot = tenant_table(
        token_ids, adapter_rank, token_lengths, adapter_slot
    )
    position = token_ids - own_first
    first_rank = tensor_index * rank_share
    low_query = scale_ranks(
        small_summed[:, keyval_cols : keyval_cols + rank_share], own_rank, first_rank
    )
    low_keyval = scale_ranks(small_summed[:, keyval_cols + rank_share :], own_rank, first_rank)
    low_both = lax.all_gather(
        jnp.concatenate([low_query, low_keyval], axis=1), "tensor", axis=1
    )
    full_query = low_both[:, :, :rank_share].reshape(block_rows, -1)
    full_keyval = low_both[:, :, rank_share:].reshape(block_rows, -1)
    wide_query = widen_slots(full_query, slot_hot)
    wide_keyval = widen_slots(full_keyval, slot_hot)
    delta_keyval = product(wide_keyval, up_keyval_all)
    keyval = small_summed[:, :keyval_cols] + delta_keyval
    kv_first_col = tensor_index * keyval_cols
    is_key = kv_first_col + jnp.arange(keyval_cols, dtype=jnp.int32) < KV_HEADS * HEAD_DIM
    kv_local = jnp.where(
        is_key[None, :], rotate_pairs(keyval, position, kv_first_col), keyval
    ).astype(jnp.bfloat16)
    kv_all = lax.all_gather(kv_local, "tensor", axis=1, tiled=True)
    heads_here = query_cols // HEAD_DIM
    group_size = HEADS // KV_HEADS
    kv_here = max(heads_here // group_size, 1)
    per_kv = heads_here // kv_here
    kv_first = tensor_index * heads_here // group_size
    key_cols = KV_HEADS * HEAD_DIM
    key_heads = lax.dynamic_slice_in_dim(
        kv_all, kv_first * HEAD_DIM, kv_here * HEAD_DIM, 1
    ).reshape(block_rows, kv_here, HEAD_DIM)
    value_heads = lax.dynamic_slice_in_dim(
        kv_all, key_cols + kv_first * HEAD_DIM, kv_here * HEAD_DIM, 1
    ).reshape(block_rows, kv_here, HEAD_DIM)
    both_heads = lax.all_gather(
        jnp.concatenate([key_heads, value_heads], axis=1), ("seq", "load"), axis=0, tiled=True
    )
    piece_keys = both_heads[:, :kv_here]
    piece_values = both_heads[:, kv_here:]
    delta_query = lax.optimization_barrier(product(wide_query, up_query_all))
    query_rows = rotate_pairs(
        query_summed + delta_query, position, tensor_index * query_cols
    ).astype(jnp.bfloat16)
    grouped = query_rows.reshape(block_rows, kv_here, per_kv, HEAD_DIM)
    key_ids = jnp.arange(piece_keys.shape[0], dtype=jnp.int32)
    visible = (key_ids[None, :] >= own_first[:, None]) & (key_ids[None, :] <= token_ids[:, None])
    scores = jnp.einsum(
        "qghd,kgd->ghqk", grouped, piece_keys, preferred_element_type=jnp.float32
    ) / math.sqrt(HEAD_DIM)
    scores = jnp.where(visible, scores, -1e30)
    row_top = jnp.max(scores, axis=3)
    exp_scores = jnp.where(visible, jnp.exp(scores - row_top[..., None]), 0.0)
    row_total = jnp.sum(exp_scores, axis=3)
    accumulated = jnp.einsum(
        "ghqk,kgd->ghqd",
        exp_scores.astype(jnp.bfloat16),
        piece_values,
        preferred_element_type=jnp.float32,
    )
    context = (accumulated / row_total[..., None]).astype(jnp.bfloat16)
    context = jnp.transpose(context, (2, 0, 1, 3)).reshape(block_rows, query_cols)
    return (context, kv_local)


def solution(mesh):
    placed = (
        P(("groups", "tensor"), ("seq", "load")),
        P(("seq", "load"), "tensor"),
        P(("seq", "load"), "tensor"),
        P(("seq", "load"), ("groups", "tensor")),
        P(("seq", "load"), ("groups", "tensor")),
        P(("groups", "load"), "tensor"),
        P(("groups", "load"), "tensor"),
        P("groups"),
        P("groups"),
        P("groups"),
    )
    return jax.shard_map(
        shards,
        mesh=mesh,
        in_specs=placed,
        out_specs=(P(("groups", "seq", "load"), "tensor"), P(("groups", "seq", "load"), "tensor")),
        check_vma=False,
    )
```

```python
import math

import jax
import jax.numpy as jnp
from jax import lax
from jax.sharding import PartitionSpec as P

HEADS = 128
KV_HEADS = 8
HEAD_DIM = 128
TENANTS = 4


ROPE_BASE = 500000.0
ADAPTER_ALPHA = 8.0


def product(left, right):
    return jnp.dot(left, right, preferred_element_type=jnp.float32)


def rotate_pairs(values, position, first_col):
    cols = values.shape[1]
    width = HEAD_DIM if cols % HEAD_DIM == 0 else cols
    col = jnp.arange(width, dtype=jnp.int32)
    pair_col = first_col + col - col % 2
    within = pair_col % HEAD_DIM // 2
    frequency = jnp.exp(-(2.0 * within.astype(jnp.float32) / HEAD_DIM) * math.log(ROPE_BASE))
    angles = position.astype(jnp.float32)[:, None] * frequency[None, :]
    cosine = jnp.cos(angles)
    sine_angle = jnp.sin(angles)
    signed_sine = jnp.where((col % 2 == 0)[None, :], -sine_angle, sine_angle)
    cosine = jnp.tile(cosine, (1, cols // width))
    signed_sine = jnp.tile(signed_sine, (1, cols // width))
    is_even = (jnp.arange(cols, dtype=jnp.int32) % 2 == 0)[None, :]
    partner = jnp.where(is_even, jnp.roll(values, -1, axis=1), jnp.roll(values, 1, axis=1))
    return values * cosine + partner * signed_sine


def tenant_table(token_ids, adapter_rank, token_lengths, adapter_slot):
    segment_ends = jnp.cumsum(token_lengths)
    begins = segment_ends - token_lengths
    owned_rows = (token_ids[:, None] >= begins[None, :]) & (
        token_ids[:, None] < segment_ends[None, :]
    )
    zero_int = jnp.zeros((), jnp.int32)
    own_rank = jnp.sum(jnp.where(owned_rows, adapter_rank[None, :], zero_int), axis=1)
    own_slot = jnp.sum(jnp.where(owned_rows, adapter_slot[None, :], zero_int), axis=1)
    own_first = jnp.sum(jnp.where(owned_rows, begins[None, :], zero_int), axis=1)
    slot_hot = own_slot[:, None] == jnp.arange(TENANTS, dtype=jnp.int32)[None, :]
    return (own_rank, own_first, slot_hot)


def select_slot(down_values, slot_hot):
    shaped = down_values.reshape(down_values.shape[0], -1, TENANTS)
    return jnp.sum(jnp.where(slot_hot[:, None, :], shaped, 0.0), axis=2)


def scale_ranks(picked, own_rank, first_rank):
    rank_index = first_rank + jnp.arange(picked.shape[1], dtype=jnp.int32)
    keep_mask = rank_index[None, :] < own_rank[:, None]
    factor = ADAPTER_ALPHA / jnp.sqrt(own_rank.astype(jnp.float32))
    return jnp.where(keep_mask, picked * factor[:, None], 0.0).astype(jnp.bfloat16)


def widen_slots(low_values, slot_hot):
    wide_rows = jnp.where(
        slot_hot[:, None, :], low_values[:, :, None], jnp.zeros((), low_values.dtype)
    )
    return wide_rows.reshape(low_values.shape[0], -1)


def ring_gather(piece, axis):
    count = lax.axis_size(axis)
    me = lax.axis_index(axis)
    if count == 1:
        return piece
    shift = [(i, (i + 1) % count) for i in range(count)]
    pieces = [piece]
    for _ in range(1, count):
        pieces.append(lax.ppermute(pieces[-1], axis, shift))
    stacked = jnp.stack(pieces)
    order = (me - jnp.arange(count, dtype=jnp.int32)) % count
    return jnp.take(stacked, order, axis=0).reshape((count * piece.shape[0],) + piece.shape[1:])


def ring_reduce_scatter(blocks, axis):
    count = lax.axis_size(axis)
    me = lax.axis_index(axis)
    if count == 1:
        return blocks[0]
    shift = [(i, (i + 1) % count) for i in range(count)]

    def pick(step):
        return lax.dynamic_index_in_dim(blocks, (me - 1 - step) % count, 0, keepdims=False)

    total = pick(0)
    for step in range(1, count):
        total = lax.ppermute(total, axis, shift) + pick(step)
    return total


def shards(
    tokens,
    weight_query,
    weight_keyval,
    down_query,
    down_keyval,
    up_query,
    up_keyval,
    adapter_rank,
    token_lengths,
    adapter_slot,
):
    tensor_count = lax.axis_size("tensor")
    block_count = lax.axis_size(("seq", "load"))
    tensor_index = lax.axis_index("tensor")
    block_index = lax.axis_index(("seq", "load"))
    query_cols = weight_query.shape[1]
    keyval_cols = weight_keyval.shape[1]
    rank_share = down_query.shape[1] // TENANTS
    block_rows = tokens.shape[0] * tensor_count // block_count
    up_query_all = ring_gather(up_query, "load")
    up_keyval_all = ring_gather(up_keyval, "load")
    ring = tensor_count
    chunk = tokens.shape[0]
    seq_count = lax.axis_size("seq")
    load_count = lax.axis_size("load")
    small_cols = keyval_cols + 2 * rank_share
    small_terms = jnp.zeros((ring, chunk, small_cols), jnp.float32)
    query_terms = jnp.zeros((ring, chunk, query_cols), jnp.float32)
    shift = [(i, (i + 1) % ring) for i in range(ring)]
    held = tokens
    for step in range(ring):
        following = lax.ppermute(held, "tensor", shift) if step < ring - 1 else None
        owner = (tensor_index - step) % ring
        block_ids = owner * chunk + jnp.arange(chunk, dtype=jnp.int32)
        _, _, block_hot = tenant_table(block_ids, adapter_rank, token_lengths, adapter_slot)
        small_block = jnp.concatenate(
            [
                product(held, weight_keyval),
                select_slot(product(held, down_query), block_hot),
                select_slot(product(held, down_keyval), block_hot),
            ],
            axis=1,
        )
        small_terms = lax.dynamic_update_slice_in_dim(small_terms, small_block[None], owner, 0)
        if step == 0 and ring > 2:
            first_block, first_owner = held, owner
        elif step == 1 and ring > 2:
            pair = product(jnp.concatenate([first_block, held], axis=0), weight_query)
            query_terms = lax.dynamic_update_slice_in_dim(
                query_terms, pair[:chunk][None], first_owner, 0
            )
            query_terms = lax.dynamic_update_slice_in_dim(
                query_terms, pair[chunk:][None], owner, 0
            )
        else:
            query_terms = lax.dynamic_update_slice_in_dim(
                query_terms, product(held, weight_query)[None], owner, 0
            )
        if following is not None:
            if step == 0 and ring > 2:
                following, small_terms, first_block = lax.optimization_barrier(
                    (following, small_terms, first_block)
                )
            else:
                following, small_terms, query_terms = lax.optimization_barrier(
                    (following, small_terms, query_terms)
                )
        held = following
    by_core = small_terms.reshape(seq_count, load_count, block_rows, -1)
    per_core = ring_reduce_scatter(jnp.moveaxis(by_core, 1, 0), "load")
    small_summed = ring_reduce_scatter(per_core, "seq")
    query_by_core = query_terms.reshape(seq_count, load_count, block_rows, -1)
    query_summed = ring_reduce_scatter(
        ring_reduce_scatter(jnp.moveaxis(query_by_core, 1, 0), "load"), "seq"
    )
    token_ids = block_index * block_rows + jnp.arange(block_rows, dtype=jnp.int32)
    own_rank, own_first, slot_hot = tenant_table(
        token_ids, adapter_rank, token_lengths, adapter_slot
    )
    position = token_ids - own_first
    first_rank = tensor_index * rank_share
    low_query = scale_ranks(
        small_summed[:, keyval_cols : keyval_cols + rank_share], own_rank, first_rank
    )
    low_keyval = scale_ranks(small_summed[:, keyval_cols + rank_share :], own_rank, first_rank)
    low_both = lax.all_gather(
        jnp.concatenate([low_query, low_keyval], axis=1), "tensor", axis=1
    )
    full_query = low_both[:, :, :rank_share].reshape(block_rows, -1)
    full_keyval = low_both[:, :, rank_share:].reshape(block_rows, -1)
    wide_query = widen_slots(full_query, slot_hot)
    wide_keyval = widen_slots(full_keyval, slot_hot)
    delta_keyval = product(wide_keyval, up_keyval_all)
    keyval = small_summed[:, :keyval_cols] + delta_keyval
    kv_first_col = tensor_index * keyval_cols
    is_key = kv_first_col + jnp.arange(keyval_cols, dtype=jnp.int32) < KV_HEADS * HEAD_DIM
    kv_local = jnp.where(
        is_key[None, :], rotate_pairs(keyval, position, kv_first_col), keyval
    ).astype(jnp.bfloat16)
    kv_all = lax.all_gather(kv_local, "tensor", axis=1, tiled=True)
    heads_here = query_cols // HEAD_DIM
    group_size = HEADS // KV_HEADS
    kv_here = max(heads_here // group_size, 1)
    per_kv = heads_here // kv_here
    kv_first = tensor_index * heads_here // group_size
    key_cols = KV_HEADS * HEAD_DIM
    key_heads = lax.dynamic_slice_in_dim(
        kv_all, kv_first * HEAD_DIM, kv_here * HEAD_DIM, 1
    ).reshape(block_rows, kv_here, HEAD_DIM)
    value_heads = lax.dynamic_slice_in_dim(
        kv_all, key_cols + kv_first * HEAD_DIM, kv_here * HEAD_DIM, 1
    ).reshape(block_rows, kv_here, HEAD_DIM)
    both_heads = lax.all_gather(
        jnp.concatenate([key_heads, value_heads], axis=1), ("seq", "load"), axis=0, tiled=True
    )
    piece_keys = both_heads[:, :kv_here]
    piece_values = both_heads[:, kv_here:]
    delta_query = lax.optimization_barrier(product(wide_query, up_query_all))
    query_rows = rotate_pairs(
        query_summed + delta_query, position, tensor_index * query_cols
    ).astype(jnp.bfloat16)
    grouped = query_rows.reshape(block_rows, kv_here, per_kv, HEAD_DIM)
    key_ids = jnp.arange(piece_keys.shape[0], dtype=jnp.int32)
    visible = (key_ids[None, :] >= own_first[:, None]) & (key_ids[None, :] <= token_ids[:, None])
    scores = jnp.einsum(
        "qghd,kgd->ghqk", grouped, piece_keys, preferred_element_type=jnp.float32
    ) / math.sqrt(HEAD_DIM)
    scores = jnp.where(visible, scores, -1e30)
    row_top = jnp.max(scores, axis=3)
    exp_scores = jnp.where(visible, jnp.exp(scores - row_top[..., None]), 0.0)
    row_total = jnp.sum(exp_scores, axis=3)
    accumulated = jnp.einsum(
        "ghqk,kgd->ghqd",
        exp_scores.astype(jnp.bfloat16),
        piece_values,
        preferred_element_type=jnp.float32,
    )
    context = (accumulated / row_total[..., None]).astype(jnp.bfloat16)
    context = jnp.transpose(context, (2, 0, 1, 3)).reshape(block_rows, query_cols)
    return (context, kv_local)


def solution(mesh):
    placed = (
        P(("groups", "tensor"), ("seq", "load")),
        P(("seq", "load"), "tensor"),
        P(("seq", "load"), "tensor"),
        P(("seq", "load"), ("groups", "tensor")),
        P(("seq", "load"), ("groups", "tensor")),
        P(("groups", "load"), "tensor"),
        P(("groups", "load"), "tensor"),
        P("groups"),
        P("groups"),
        P("groups"),
    )
    return jax.shard_map(
        shards,
        mesh=mesh,
        in_specs=placed,
        out_specs=(P(("groups", "seq", "load"), "tensor"), P(("groups", "seq", "load"), "tensor")),
        check_vma=False,
    )
```

```python
import math

import jax
import jax.numpy as jnp
from jax import lax
from jax.sharding import PartitionSpec as P

HEADS = 128
KV_HEADS = 8
HEAD_DIM = 128
TENANTS = 4


ROPE_BASE = 500000.0
ADAPTER_ALPHA = 8.0


def product(left, right):
    return jnp.dot(left, right, preferred_element_type=jnp.float32)


def rotate_pairs(values, position, first_col):
    cols = values.shape[1]
    width = HEAD_DIM if cols % HEAD_DIM == 0 else cols
    col = jnp.arange(width, dtype=jnp.int32)
    pair_col = first_col + col - col % 2
    within = pair_col % HEAD_DIM // 2
    frequency = jnp.exp(-(2.0 * within.astype(jnp.float32) / HEAD_DIM) * math.log(ROPE_BASE))
    angles = position.astype(jnp.float32)[:, None] * frequency[None, :]
    cosine = jnp.cos(angles)
    sine_angle = jnp.sin(angles)
    signed_sine = jnp.where((col % 2 == 0)[None, :], -sine_angle, sine_angle)
    cosine = jnp.tile(cosine, (1, cols // width))
    signed_sine = jnp.tile(signed_sine, (1, cols // width))
    is_even = (jnp.arange(cols, dtype=jnp.int32) % 2 == 0)[None, :]
    partner = jnp.where(is_even, jnp.roll(values, -1, axis=1), jnp.roll(values, 1, axis=1))
    return values * cosine + partner * signed_sine


def tenant_table(token_ids, adapter_rank, token_lengths, adapter_slot):
    segment_ends = jnp.cumsum(token_lengths)
    begins = segment_ends - token_lengths
    owned_rows = (token_ids[:, None] >= begins[None, :]) & (
        token_ids[:, None] < segment_ends[None, :]
    )
    zero_int = jnp.zeros((), jnp.int32)
    own_rank = jnp.sum(jnp.where(owned_rows, adapter_rank[None, :], zero_int), axis=1)
    own_slot = jnp.sum(jnp.where(owned_rows, adapter_slot[None, :], zero_int), axis=1)
    own_first = jnp.sum(jnp.where(owned_rows, begins[None, :], zero_int), axis=1)
    slot_hot = own_slot[:, None] == jnp.arange(TENANTS, dtype=jnp.int32)[None, :]
    return (own_rank, own_first, slot_hot)


def select_slot(down_values, slot_hot):
    shaped = down_values.reshape(down_values.shape[0], -1, TENANTS)
    return jnp.sum(jnp.where(slot_hot[:, None, :], shaped, 0.0), axis=2)


def scale_ranks(picked, own_rank, first_rank):
    rank_index = first_rank + jnp.arange(picked.shape[1], dtype=jnp.int32)
    keep_mask = rank_index[None, :] < own_rank[:, None]
    factor = ADAPTER_ALPHA / jnp.sqrt(own_rank.astype(jnp.float32))
    return jnp.where(keep_mask, picked * factor[:, None], 0.0).astype(jnp.bfloat16)


def widen_slots(low_values, slot_hot):
    wide_rows = jnp.where(
        slot_hot[:, None, :], low_values[:, :, None], jnp.zeros((), low_values.dtype)
    )
    return wide_rows.reshape(low_values.shape[0], -1)


def ring_reduce_scatter(blocks, axis):
    count = lax.axis_size(axis)
    me = lax.axis_index(axis)
    if count == 1:
        return blocks[0]
    shift = [(i, (i + 1) % count) for i in range(count)]

    def pick(step):
        return lax.dynamic_index_in_dim(blocks, (me - 1 - step) % count, 0, keepdims=False)

    total = pick(0)
    for step in range(1, count):
        total = lax.ppermute(total, axis, shift) + pick(step)
    return total


def shards(
    tokens,
    weight_query,
    weight_keyval,
    down_query,
    down_keyval,
    up_query,
    up_keyval,
    adapter_rank,
    token_lengths,
    adapter_slot,
):
    tensor_count = lax.axis_size("tensor")
    block_count = lax.axis_size(("seq", "load"))
    tensor_index = lax.axis_index("tensor")
    block_index = lax.axis_index(("seq", "load"))
    query_cols = weight_query.shape[1]
    keyval_cols = weight_keyval.shape[1]
    rank_share = down_query.shape[1] // TENANTS
    block_rows = tokens.shape[0] * tensor_count // block_count
    up_query_all = lax.all_gather(up_query, "load", axis=0, tiled=True)
    up_keyval_all = lax.all_gather(up_keyval, "load", axis=0, tiled=True)
    ring = tensor_count
    chunk = tokens.shape[0]
    small_cols = keyval_cols + 2 * rank_share
    small_terms = jnp.zeros((ring, chunk, small_cols), jnp.float32)
    query_terms = jnp.zeros((ring, chunk, query_cols), jnp.float32)
    shift = [(i, (i + 1) % ring) for i in range(ring)]
    held = tokens
    waiting = []
    for step in range(ring):
        following = lax.ppermute(held, "tensor", shift) if step < ring - 1 else None
        owner = (tensor_index - step) % ring
        defer = 0 < step < ring - 1 and ring <= 4
        if defer:
            waiting.append((held, owner))
        else:
            batch = waiting + [(held, owner)] if step == ring - 1 else [(held, owner)]
            rows_now = jnp.concatenate([b for b, _ in batch], axis=0)
            block_ids = jnp.concatenate(
                [o * chunk + jnp.arange(chunk, dtype=jnp.int32) for _, o in batch]
            )
            _, _, block_hot = tenant_table(block_ids, adapter_rank, token_lengths, adapter_slot)
            small_rows = jnp.concatenate(
                [
                    product(rows_now, weight_keyval),
                    select_slot(product(rows_now, down_query), block_hot),
                    select_slot(product(rows_now, down_keyval), block_hot),
                ],
                axis=1,
            )
            for index, (_, o) in enumerate(batch):
                small_terms = lax.dynamic_update_slice_in_dim(
                    small_terms, small_rows[index * chunk : (index + 1) * chunk][None], o, 0
                )
        if step == 0 and ring > 2:
            first_block, first_owner = held, owner
        elif step == 1 and ring > 2:
            pair = product(jnp.concatenate([first_block, held], axis=0), weight_query)
            query_terms = lax.dynamic_update_slice_in_dim(
                query_terms, pair[:chunk][None], first_owner, 0
            )
            query_terms = lax.dynamic_update_slice_in_dim(
                query_terms, pair[chunk:][None], owner, 0
            )
        else:
            query_terms = lax.dynamic_update_slice_in_dim(
                query_terms, product(held, weight_query)[None], owner, 0
            )
        if following is not None:
            if step == 0 and ring > 2:
                following, small_terms, first_block = lax.optimization_barrier(
                    (following, small_terms, first_block)
                )
            else:
                following, small_terms, query_terms = lax.optimization_barrier(
                    (following, small_terms, query_terms)
                )
        held = following
    seq_count = lax.axis_size("seq")
    load_count = lax.axis_size("load")
    by_core = small_terms.reshape(seq_count, load_count, block_rows, -1)
    per_core = ring_reduce_scatter(jnp.moveaxis(by_core, 1, 0), "load")
    small_summed = ring_reduce_scatter(per_core, "seq")
    query_summed = lax.psum_scatter(
        query_terms.reshape(ring * chunk, -1), ("seq", "load"), scatter_dimension=0, tiled=True
    )
    token_ids = block_index * block_rows + jnp.arange(block_rows, dtype=jnp.int32)
    own_rank, own_first, slot_hot = tenant_table(
        token_ids, adapter_rank, token_lengths, adapter_slot
    )
    position = token_ids - own_first
    first_rank = tensor_index * rank_share
    low_query = scale_ranks(
        small_summed[:, keyval_cols : keyval_cols + rank_share], own_rank, first_rank
    )
    low_keyval = scale_ranks(small_summed[:, keyval_cols + rank_share :], own_rank, first_rank)
    low_both = lax.all_gather(
        jnp.concatenate([low_query, low_keyval], axis=1), "tensor", axis=1
    )
    full_query = low_both[:, :, :rank_share].reshape(block_rows, -1)
    full_keyval = low_both[:, :, rank_share:].reshape(block_rows, -1)
    wide_query = widen_slots(full_query, slot_hot)
    wide_keyval = widen_slots(full_keyval, slot_hot)
    delta_keyval = product(wide_keyval, up_keyval_all)
    keyval = small_summed[:, :keyval_cols] + delta_keyval
    kv_first_col = tensor_index * keyval_cols
    is_key = kv_first_col + jnp.arange(keyval_cols, dtype=jnp.int32) < KV_HEADS * HEAD_DIM
    kv_local = jnp.where(
        is_key[None, :], rotate_pairs(keyval, position, kv_first_col), keyval
    ).astype(jnp.bfloat16)
    kv_all = lax.all_gather(kv_local, "tensor", axis=1, tiled=True)
    heads_here = query_cols // HEAD_DIM
    group_size = HEADS // KV_HEADS
    kv_here = max(heads_here // group_size, 1)
    per_kv = heads_here // kv_here
    kv_first = tensor_index * heads_here // group_size
    key_cols = KV_HEADS * HEAD_DIM
    key_heads = lax.dynamic_slice_in_dim(
        kv_all, kv_first * HEAD_DIM, kv_here * HEAD_DIM, 1
    ).reshape(block_rows, kv_here, HEAD_DIM)
    value_heads = lax.dynamic_slice_in_dim(
        kv_all, key_cols + kv_first * HEAD_DIM, kv_here * HEAD_DIM, 1
    ).reshape(block_rows, kv_here, HEAD_DIM)
    both_heads = lax.all_gather(
        jnp.concatenate([key_heads, value_heads], axis=1), ("seq", "load"), axis=0, tiled=True
    )
    piece_keys = both_heads[:, :kv_here]
    piece_values = both_heads[:, kv_here:]
    delta_query = lax.optimization_barrier(product(wide_query, up_query_all))
    query_rows = rotate_pairs(
        query_summed + delta_query, position, tensor_index * query_cols
    ).astype(jnp.bfloat16)
    grouped = query_rows.reshape(block_rows, kv_here, per_kv, HEAD_DIM)
    key_ids = jnp.arange(piece_keys.shape[0], dtype=jnp.int32)
    visible = (key_ids[None, :] >= own_first[:, None]) & (key_ids[None, :] <= token_ids[:, None])
    scores = jnp.einsum(
        "qghd,kgd->ghqk", grouped, piece_keys, preferred_element_type=jnp.float32
    ) / math.sqrt(HEAD_DIM)
    scores = jnp.where(visible, scores, -1e30)
    row_top = jnp.max(scores, axis=3)
    exp_scores = jnp.where(visible, jnp.exp(scores - row_top[..., None]), 0.0)
    row_total = jnp.sum(exp_scores, axis=3)
    accumulated = jnp.einsum(
        "ghqk,kgd->ghqd",
        exp_scores.astype(jnp.bfloat16),
        piece_values,
        preferred_element_type=jnp.float32,
    )
    context = (accumulated / row_total[..., None]).astype(jnp.bfloat16)
    context = jnp.transpose(context, (2, 0, 1, 3)).reshape(block_rows, query_cols)
    return (context, kv_local)


def solution(mesh):
    placed = (
        P(("groups", "tensor"), ("seq", "load")),
        P(("seq", "load"), "tensor"),
        P(("seq", "load"), "tensor"),
        P(("seq", "load"), ("groups", "tensor")),
        P(("seq", "load"), ("groups", "tensor")),
        P(("groups", "load"), "tensor"),
        P(("groups", "load"), "tensor"),
        P("groups"),
        P("groups"),
        P("groups"),
    )
    return jax.shard_map(
        shards,
        mesh=mesh,
        in_specs=placed,
        out_specs=(P(("groups", "seq", "load"), "tensor"), P(("groups", "seq", "load"), "tensor")),
        check_vma=False,
    )
```

```python
import math

import jax
import jax.numpy as jnp
from jax import lax
from jax.sharding import PartitionSpec as P

HEADS = 128
KV_HEADS = 8
HEAD_DIM = 128
TENANTS = 4


ROPE_BASE = 500000.0
ADAPTER_ALPHA = 8.0


def product(left, right):
    return jnp.dot(left, right, preferred_element_type=jnp.float32)


def rotate_pairs(values, position, first_col):
    cols = values.shape[1]
    width = HEAD_DIM if cols % HEAD_DIM == 0 else cols
    col = jnp.arange(width, dtype=jnp.int32)
    pair_col = first_col + col - col % 2
    within = pair_col % HEAD_DIM // 2
    frequency = jnp.exp(-(2.0 * within.astype(jnp.float32) / HEAD_DIM) * math.log(ROPE_BASE))
    angles = position.astype(jnp.float32)[:, None] * frequency[None, :]
    cosine = jnp.cos(angles)
    sine_angle = jnp.sin(angles)
    signed_sine = jnp.where((col % 2 == 0)[None, :], -sine_angle, sine_angle)
    cosine, signed_sine = lax.optimization_barrier((cosine, signed_sine))
    cosine = jnp.tile(cosine, (1, cols // width))
    signed_sine = jnp.tile(signed_sine, (1, cols // width))
    is_even = (jnp.arange(cols, dtype=jnp.int32) % 2 == 0)[None, :]
    partner = jnp.where(is_even, jnp.roll(values, -1, axis=1), jnp.roll(values, 1, axis=1))
    return values * cosine + partner * signed_sine


def tenant_table(token_ids, adapter_rank, token_lengths, adapter_slot):
    segment_ends = jnp.cumsum(token_lengths)
    begins = segment_ends - token_lengths
    owned_rows = (token_ids[:, None] >= begins[None, :]) & (
        token_ids[:, None] < segment_ends[None, :]
    )
    zero_int = jnp.zeros((), jnp.int32)
    own_rank = jnp.sum(jnp.where(owned_rows, adapter_rank[None, :], zero_int), axis=1)
    own_slot = jnp.sum(jnp.where(owned_rows, adapter_slot[None, :], zero_int), axis=1)
    own_first = jnp.sum(jnp.where(owned_rows, begins[None, :], zero_int), axis=1)
    slot_hot = own_slot[:, None] == jnp.arange(TENANTS, dtype=jnp.int32)[None, :]
    return (own_rank, own_first, slot_hot)


def select_slot(down_values, slot_hot):
    shaped = down_values.reshape(down_values.shape[0], -1, TENANTS)
    return jnp.sum(jnp.where(slot_hot[:, None, :], shaped, 0.0), axis=2)


def scale_ranks(picked, own_rank, first_rank):
    rank_index = first_rank + jnp.arange(picked.shape[1], dtype=jnp.int32)
    keep_mask = rank_index[None, :] < own_rank[:, None]
    factor = ADAPTER_ALPHA / jnp.sqrt(own_rank.astype(jnp.float32))
    return jnp.where(keep_mask, picked * factor[:, None], 0.0).astype(jnp.bfloat16)


def widen_slots(low_values, slot_hot):
    wide_rows = jnp.where(
        slot_hot[:, None, :], low_values[:, :, None], jnp.zeros((), low_values.dtype)
    )
    return wide_rows.reshape(low_values.shape[0], -1)


def ring_reduce_scatter(blocks, axis):
    count = lax.axis_size(axis)
    me = lax.axis_index(axis)
    if count == 1:
        return blocks[0]
    shift = [(i, (i + 1) % count) for i in range(count)]

    def pick(step):
        return lax.dynamic_index_in_dim(blocks, (me - 1 - step) % count, 0, keepdims=False)

    total = pick(0)
    for step in range(1, count):
        total = lax.ppermute(total, axis, shift) + pick(step)
    return total


def shards(
    tokens,
    weight_query,
    weight_keyval,
    down_query,
    down_keyval,
    up_query,
    up_keyval,
    adapter_rank,
    token_lengths,
    adapter_slot,
):
    tensor_count = lax.axis_size("tensor")
    block_count = lax.axis_size(("seq", "load"))
    tensor_index = lax.axis_index("tensor")
    block_index = lax.axis_index(("seq", "load"))
    query_cols = weight_query.shape[1]
    keyval_cols = weight_keyval.shape[1]
    rank_share = down_query.shape[1] // TENANTS
    block_rows = tokens.shape[0] * tensor_count // block_count
    up_query_all = lax.all_gather(up_query, "load", axis=0, tiled=True)
    up_keyval_all = lax.all_gather(up_keyval, "load", axis=0, tiled=True)
    ring = tensor_count
    chunk = tokens.shape[0]
    small_cols = keyval_cols + 2 * rank_share
    small_terms = jnp.zeros((ring, chunk, small_cols), jnp.float32)
    query_terms = jnp.zeros((ring, chunk, query_cols), jnp.float32)
    shift = [(i, (i + 1) % ring) for i in range(ring)]
    held = tokens
    for step in range(ring):
        following = lax.ppermute(held, "tensor", shift) if step < ring - 1 else None
        owner = (tensor_index - step) % ring
        block_ids = owner * chunk + jnp.arange(chunk, dtype=jnp.int32)
        _, _, block_hot = tenant_table(block_ids, adapter_rank, token_lengths, adapter_slot)
        small_block = jnp.concatenate(
            [
                product(held, weight_keyval),
                select_slot(product(held, down_query), block_hot),
                select_slot(product(held, down_keyval), block_hot),
            ],
            axis=1,
        )
        small_terms = lax.dynamic_update_slice_in_dim(small_terms, small_block[None], owner, 0)
        if step == 0 and ring > 2:
            first_block, first_owner = held, owner
        elif step == 1 and ring > 2:
            pair = product(jnp.concatenate([first_block, held], axis=0), weight_query)
            query_terms = lax.dynamic_update_slice_in_dim(
                query_terms, pair[:chunk][None], first_owner, 0
            )
            query_terms = lax.dynamic_update_slice_in_dim(
                query_terms, pair[chunk:][None], owner, 0
            )
        else:
            query_terms = lax.dynamic_update_slice_in_dim(
                query_terms, product(held, weight_query)[None], owner, 0
            )
        if following is not None:
            if step == 0 and ring > 2:
                following, small_terms, first_block = lax.optimization_barrier(
                    (following, small_terms, first_block)
                )
            else:
                following, small_terms, query_terms = lax.optimization_barrier(
                    (following, small_terms, query_terms)
                )
        held = following
    seq_count = lax.axis_size("seq")
    load_count = lax.axis_size("load")
    by_core = small_terms.reshape(seq_count, load_count, block_rows, -1)
    per_core = ring_reduce_scatter(jnp.moveaxis(by_core, 1, 0), "load")
    small_summed = ring_reduce_scatter(per_core, "seq")
    query_summed = lax.psum_scatter(
        query_terms.reshape(ring * chunk, -1), ("seq", "load"), scatter_dimension=0, tiled=True
    )
    token_ids = block_index * block_rows + jnp.arange(block_rows, dtype=jnp.int32)
    own_rank, own_first, slot_hot = tenant_table(
        token_ids, adapter_rank, token_lengths, adapter_slot
    )
    position = token_ids - own_first
    first_rank = tensor_index * rank_share
    low_query = scale_ranks(
        small_summed[:, keyval_cols : keyval_cols + rank_share], own_rank, first_rank
    )
    low_keyval = scale_ranks(small_summed[:, keyval_cols + rank_share :], own_rank, first_rank)
    low_both = lax.all_gather(
        jnp.concatenate([low_query, low_keyval], axis=1), "tensor", axis=1
    )
    full_query = low_both[:, :, :rank_share].reshape(block_rows, -1)
    full_keyval = low_both[:, :, rank_share:].reshape(block_rows, -1)
    wide_query = widen_slots(full_query, slot_hot)
    wide_keyval = widen_slots(full_keyval, slot_hot)
    delta_keyval = product(wide_keyval, up_keyval_all)
    keyval = small_summed[:, :keyval_cols] + delta_keyval
    kv_first_col = tensor_index * keyval_cols
    is_key = kv_first_col + jnp.arange(keyval_cols, dtype=jnp.int32) < KV_HEADS * HEAD_DIM
    kv_local = jnp.where(
        is_key[None, :], rotate_pairs(keyval, position, kv_first_col), keyval
    ).astype(jnp.bfloat16)
    kv_all = lax.all_gather(kv_local, "tensor", axis=1, tiled=True)
    heads_here = query_cols // HEAD_DIM
    group_size = HEADS // KV_HEADS
    kv_here = max(heads_here // group_size, 1)
    per_kv = heads_here // kv_here
    kv_first = tensor_index * heads_here // group_size
    key_cols = KV_HEADS * HEAD_DIM
    key_heads = lax.dynamic_slice_in_dim(
        kv_all, kv_first * HEAD_DIM, kv_here * HEAD_DIM, 1
    ).reshape(block_rows, kv_here, HEAD_DIM)
    value_heads = lax.dynamic_slice_in_dim(
        kv_all, key_cols + kv_first * HEAD_DIM, kv_here * HEAD_DIM, 1
    ).reshape(block_rows, kv_here, HEAD_DIM)
    both_heads = lax.all_gather(
        jnp.concatenate([key_heads, value_heads], axis=1), ("seq", "load"), axis=0, tiled=True
    )
    piece_keys = both_heads[:, :kv_here]
    piece_values = both_heads[:, kv_here:]
    delta_query = lax.optimization_barrier(product(wide_query, up_query_all))
    query_rows = rotate_pairs(
        query_summed + delta_query, position, tensor_index * query_cols
    ).astype(jnp.bfloat16)
    grouped = query_rows.reshape(block_rows, kv_here, per_kv, HEAD_DIM)
    key_ids = jnp.arange(piece_keys.shape[0], dtype=jnp.int32)
    visible = (key_ids[None, :] >= own_first[:, None]) & (key_ids[None, :] <= token_ids[:, None])
    scores = jnp.einsum(
        "qghd,kgd->ghqk", grouped, piece_keys, preferred_element_type=jnp.float32
    ) / math.sqrt(HEAD_DIM)
    scores = jnp.where(visible, scores, -1e30)
    row_top = jnp.max(scores, axis=3)
    exp_scores = jnp.where(visible, jnp.exp(scores - row_top[..., None]), 0.0)
    row_total = jnp.sum(exp_scores, axis=3)
    accumulated = jnp.einsum(
        "ghqk,kgd->ghqd",
        exp_scores.astype(jnp.bfloat16),
        piece_values,
        preferred_element_type=jnp.float32,
    )
    context = (accumulated / row_total[..., None]).astype(jnp.bfloat16)
    context = jnp.transpose(context, (2, 0, 1, 3)).reshape(block_rows, query_cols)
    return (context, kv_local)


def solution(mesh):
    placed = (
        P(("groups", "tensor"), ("seq", "load")),
        P(("seq", "load"), "tensor"),
        P(("seq", "load"), "tensor"),
        P(("seq", "load"), ("groups", "tensor")),
        P(("seq", "load"), ("groups", "tensor")),
        P(("groups", "load"), "tensor"),
        P(("groups", "load"), "tensor"),
        P("groups"),
        P("groups"),
        P("groups"),
    )
    return jax.shard_map(
        shards,
        mesh=mesh,
        in_specs=placed,
        out_specs=(P(("groups", "seq", "load"), "tensor"), P(("groups", "seq", "load"), "tensor")),
        check_vma=False,
    )
```

```python
import math

import jax
import jax.numpy as jnp
from jax import lax
from jax.sharding import PartitionSpec as P

HEADS = 128
KV_HEADS = 8
HEAD_DIM = 128
TENANTS = 4


ROPE_BASE = 500000.0
ADAPTER_ALPHA = 8.0


def product(left, right):
    return jnp.dot(left, right, preferred_element_type=jnp.float32)


def rotate_pairs(values, position, first_col):
    cols = values.shape[1]
    width = HEAD_DIM if cols % HEAD_DIM == 0 else cols
    col = jnp.arange(width, dtype=jnp.int32)
    pair_col = first_col + col - col % 2
    within = pair_col % HEAD_DIM // 2
    frequency = jnp.exp(-(2.0 * within.astype(jnp.float32) / HEAD_DIM) * math.log(ROPE_BASE))
    angles = position.astype(jnp.float32)[:, None] * frequency[None, :]
    cosine = jnp.cos(angles)
    sine_angle = jnp.sin(angles)
    signed_sine = jnp.where((col % 2 == 0)[None, :], -sine_angle, sine_angle)
    cosine, signed_sine = lax.optimization_barrier((cosine, signed_sine))
    cosine = jnp.tile(cosine, (1, cols // width))
    signed_sine = jnp.tile(signed_sine, (1, cols // width))
    is_even = (jnp.arange(cols, dtype=jnp.int32) % 2 == 0)[None, :]
    partner = jnp.where(is_even, jnp.roll(values, -1, axis=1), jnp.roll(values, 1, axis=1))
    return values * cosine + partner * signed_sine


def tenant_table(token_ids, adapter_rank, token_lengths, adapter_slot):
    segment_ends = jnp.cumsum(token_lengths)
    begins = segment_ends - token_lengths
    owned_rows = (token_ids[:, None] >= begins[None, :]) & (
        token_ids[:, None] < segment_ends[None, :]
    )
    zero_int = jnp.zeros((), jnp.int32)
    own_rank = jnp.sum(jnp.where(owned_rows, adapter_rank[None, :], zero_int), axis=1)
    own_slot = jnp.sum(jnp.where(owned_rows, adapter_slot[None, :], zero_int), axis=1)
    own_first = jnp.sum(jnp.where(owned_rows, begins[None, :], zero_int), axis=1)
    slot_hot = own_slot[:, None] == jnp.arange(TENANTS, dtype=jnp.int32)[None, :]
    return (own_rank, own_first, slot_hot)


def select_slot(down_values, slot_hot):
    shaped = down_values.reshape(down_values.shape[0], -1, TENANTS)
    return jnp.sum(jnp.where(slot_hot[:, None, :], shaped, 0.0), axis=2)


def scale_ranks(picked, own_rank, first_rank):
    rank_index = first_rank + jnp.arange(picked.shape[1], dtype=jnp.int32)
    keep_mask = rank_index[None, :] < own_rank[:, None]
    factor = ADAPTER_ALPHA / jnp.sqrt(own_rank.astype(jnp.float32))
    return jnp.where(keep_mask, picked * factor[:, None], 0.0).astype(jnp.bfloat16)


def widen_slots(low_values, slot_hot):
    wide_rows = jnp.where(
        slot_hot[:, None, :], low_values[:, :, None], jnp.zeros((), low_values.dtype)
    )
    return wide_rows.reshape(low_values.shape[0], -1)


def ring_gather(piece, axis):
    count = lax.axis_size(axis)
    me = lax.axis_index(axis)
    if count == 1:
        return piece
    shift = [(i, (i + 1) % count) for i in range(count)]
    pieces = [piece]
    for _ in range(1, count):
        pieces.append(lax.ppermute(pieces[-1], axis, shift))
    stacked = jnp.stack(pieces)
    order = (me - jnp.arange(count, dtype=jnp.int32)) % count
    return jnp.take(stacked, order, axis=0).reshape((count * piece.shape[0],) + piece.shape[1:])


def ring_reduce_scatter(blocks, axis):
    count = lax.axis_size(axis)
    me = lax.axis_index(axis)
    if count == 1:
        return blocks[0]
    shift = [(i, (i + 1) % count) for i in range(count)]

    def pick(step):
        return lax.dynamic_index_in_dim(blocks, (me - 1 - step) % count, 0, keepdims=False)

    total = pick(0)
    for step in range(1, count):
        total = lax.ppermute(total, axis, shift) + pick(step)
    return total


def shards(
    tokens,
    weight_query,
    weight_keyval,
    down_query,
    down_keyval,
    up_query,
    up_keyval,
    adapter_rank,
    token_lengths,
    adapter_slot,
):
    tensor_count = lax.axis_size("tensor")
    block_count = lax.axis_size(("seq", "load"))
    tensor_index = lax.axis_index("tensor")
    block_index = lax.axis_index(("seq", "load"))
    query_cols = weight_query.shape[1]
    keyval_cols = weight_keyval.shape[1]
    rank_share = down_query.shape[1] // TENANTS
    block_rows = tokens.shape[0] * tensor_count // block_count
    up_query_all = lax.all_gather(up_query, "load", axis=0, tiled=True)
    up_keyval_all = lax.all_gather(up_keyval, "load", axis=0, tiled=True)
    ring = tensor_count
    chunk = tokens.shape[0]
    small_cols = keyval_cols + 2 * rank_share
    small_terms = jnp.zeros((ring, chunk, small_cols), jnp.float32)
    query_terms = jnp.zeros((ring, chunk, query_cols), jnp.float32)
    shift = [(i, (i + 1) % ring) for i in range(ring)]
    held = tokens
    waiting = []
    for step in range(ring):
        following = lax.ppermute(held, "tensor", shift) if step < ring - 1 else None
        owner = (tensor_index - step) % ring
        defer = 0 < step < ring - 1 and ring <= 4
        if defer:
            waiting.append((held, owner))
        else:
            batch = waiting + [(held, owner)] if step == ring - 1 else [(held, owner)]
            rows_now = jnp.concatenate([b for b, _ in batch], axis=0)
            block_ids = jnp.concatenate(
                [o * chunk + jnp.arange(chunk, dtype=jnp.int32) for _, o in batch]
            )
            _, _, block_hot = tenant_table(block_ids, adapter_rank, token_lengths, adapter_slot)
            small_rows = jnp.concatenate(
                [
                    product(rows_now, weight_keyval),
                    select_slot(product(rows_now, down_query), block_hot),
                    select_slot(product(rows_now, down_keyval), block_hot),
                ],
                axis=1,
            )
            for index, (_, o) in enumerate(batch):
                small_terms = lax.dynamic_update_slice_in_dim(
                    small_terms, small_rows[index * chunk : (index + 1) * chunk][None], o, 0
                )
        if step == 0 and ring > 2:
            first_block, first_owner = held, owner
        elif step == 1 and ring > 2:
            pair = product(jnp.concatenate([first_block, held], axis=0), weight_query)
            query_terms = lax.dynamic_update_slice_in_dim(
                query_terms, pair[:chunk][None], first_owner, 0
            )
            query_terms = lax.dynamic_update_slice_in_dim(
                query_terms, pair[chunk:][None], owner, 0
            )
        else:
            query_terms = lax.dynamic_update_slice_in_dim(
                query_terms, product(held, weight_query)[None], owner, 0
            )
        if following is not None:
            if step == 0 and ring > 2:
                following, small_terms, first_block = lax.optimization_barrier(
                    (following, small_terms, first_block)
                )
            else:
                following, small_terms, query_terms = lax.optimization_barrier(
                    (following, small_terms, query_terms)
                )
        held = following
    seq_count = lax.axis_size("seq")
    load_count = lax.axis_size("load")
    by_core = small_terms.reshape(seq_count, load_count, block_rows, -1)
    per_core = ring_reduce_scatter(jnp.moveaxis(by_core, 1, 0), "load")
    small_summed = ring_reduce_scatter(per_core, "seq")
    query_summed = lax.psum_scatter(
        query_terms.reshape(ring * chunk, -1), ("seq", "load"), scatter_dimension=0, tiled=True
    )
    token_ids = block_index * block_rows + jnp.arange(block_rows, dtype=jnp.int32)
    own_rank, own_first, slot_hot = tenant_table(
        token_ids, adapter_rank, token_lengths, adapter_slot
    )
    position = token_ids - own_first
    first_rank = tensor_index * rank_share
    low_query = scale_ranks(
        small_summed[:, keyval_cols : keyval_cols + rank_share], own_rank, first_rank
    )
    low_keyval = scale_ranks(small_summed[:, keyval_cols + rank_share :], own_rank, first_rank)
    low_both = jnp.moveaxis(
        ring_gather(jnp.concatenate([low_query, low_keyval], axis=1)[None], "tensor"), 0, 1
    )
    full_query = low_both[:, :, :rank_share].reshape(block_rows, -1)
    full_keyval = low_both[:, :, rank_share:].reshape(block_rows, -1)
    wide_query = widen_slots(full_query, slot_hot)
    wide_keyval = widen_slots(full_keyval, slot_hot)
    delta_keyval = product(wide_keyval, up_keyval_all)
    keyval = small_summed[:, :keyval_cols] + delta_keyval
    kv_first_col = tensor_index * keyval_cols
    is_key = kv_first_col + jnp.arange(keyval_cols, dtype=jnp.int32) < KV_HEADS * HEAD_DIM
    kv_local = jnp.where(
        is_key[None, :], rotate_pairs(keyval, position, kv_first_col), keyval
    ).astype(jnp.bfloat16)
    kv_all = lax.all_gather(kv_local, "tensor", axis=1, tiled=True)
    heads_here = query_cols // HEAD_DIM
    group_size = HEADS // KV_HEADS
    kv_here = max(heads_here // group_size, 1)
    per_kv = heads_here // kv_here
    kv_first = tensor_index * heads_here // group_size
    key_cols = KV_HEADS * HEAD_DIM
    key_heads = lax.dynamic_slice_in_dim(
        kv_all, kv_first * HEAD_DIM, kv_here * HEAD_DIM, 1
    ).reshape(block_rows, kv_here, HEAD_DIM)
    value_heads = lax.dynamic_slice_in_dim(
        kv_all, key_cols + kv_first * HEAD_DIM, kv_here * HEAD_DIM, 1
    ).reshape(block_rows, kv_here, HEAD_DIM)
    both_heads = lax.all_gather(
        jnp.concatenate([key_heads, value_heads], axis=1), ("seq", "load"), axis=0, tiled=True
    )
    piece_keys = both_heads[:, :kv_here]
    piece_values = both_heads[:, kv_here:]
    delta_query = lax.optimization_barrier(product(wide_query, up_query_all))
    query_rows = rotate_pairs(
        query_summed + delta_query, position, tensor_index * query_cols
    ).astype(jnp.bfloat16)
    grouped = query_rows.reshape(block_rows, kv_here, per_kv, HEAD_DIM)
    key_ids = jnp.arange(piece_keys.shape[0], dtype=jnp.int32)
    visible = (key_ids[None, :] >= own_first[:, None]) & (key_ids[None, :] <= token_ids[:, None])
    scores = jnp.einsum(
        "qghd,kgd->ghqk", grouped, piece_keys, preferred_element_type=jnp.float32
    ) / math.sqrt(HEAD_DIM)
    scores = jnp.where(visible, scores, -1e30)
    row_top = jnp.max(scores, axis=3)
    exp_scores = jnp.where(visible, jnp.exp(scores - row_top[..., None]), 0.0)
    row_total = jnp.sum(exp_scores, axis=3)
    accumulated = jnp.einsum(
        "ghqk,kgd->ghqd",
        exp_scores.astype(jnp.bfloat16),
        piece_values,
        preferred_element_type=jnp.float32,
    )
    context = (accumulated / row_total[..., None]).astype(jnp.bfloat16)
    context = jnp.transpose(context, (2, 0, 1, 3)).reshape(block_rows, query_cols)
    return (context, kv_local)


def solution(mesh):
    placed = (
        P(("groups", "tensor"), ("seq", "load")),
        P(("seq", "load"), "tensor"),
        P(("seq", "load"), "tensor"),
        P(("seq", "load"), ("groups", "tensor")),
        P(("seq", "load"), ("groups", "tensor")),
        P(("groups", "load"), "tensor"),
        P(("groups", "load"), "tensor"),
        P("groups"),
        P("groups"),
        P("groups"),
    )
    return jax.shard_map(
        shards,
        mesh=mesh,
        in_specs=placed,
        out_specs=(P(("groups", "seq", "load"), "tensor"), P(("groups", "seq", "load"), "tensor")),
        check_vma=False,
    )
```

```python
import math

import jax
import jax.numpy as jnp
from jax import lax
from jax.sharding import PartitionSpec as P

HEADS = 128
KV_HEADS = 8
HEAD_DIM = 128
TENANTS = 4


ROPE_BASE = 500000.0
ADAPTER_ALPHA = 8.0


def product(left, right):
    return jnp.dot(left, right, preferred_element_type=jnp.float32)


def rotate_pairs(values, position, first_col):
    cols = values.shape[1]
    width = HEAD_DIM if cols % HEAD_DIM == 0 else cols
    col = jnp.arange(width, dtype=jnp.int32)
    pair_col = first_col + col - col % 2
    within = pair_col % HEAD_DIM // 2
    frequency = jnp.exp(-(2.0 * within.astype(jnp.float32) / HEAD_DIM) * math.log(ROPE_BASE))
    angles = position.astype(jnp.float32)[:, None] * frequency[None, :]
    cosine = jnp.cos(angles)
    sine_angle = jnp.sin(angles)
    signed_sine = jnp.where((col % 2 == 0)[None, :], -sine_angle, sine_angle)
    cosine, signed_sine = lax.optimization_barrier((cosine, signed_sine))
    cosine = jnp.tile(cosine, (1, cols // width))
    signed_sine = jnp.tile(signed_sine, (1, cols // width))
    is_even = (jnp.arange(cols, dtype=jnp.int32) % 2 == 0)[None, :]
    partner = jnp.where(is_even, jnp.roll(values, -1, axis=1), jnp.roll(values, 1, axis=1))
    return values * cosine + partner * signed_sine


def tenant_table(token_ids, adapter_rank, token_lengths, adapter_slot):
    segment_ends = jnp.cumsum(token_lengths)
    begins = segment_ends - token_lengths
    owned_rows = (token_ids[:, None] >= begins[None, :]) & (
        token_ids[:, None] < segment_ends[None, :]
    )
    zero_int = jnp.zeros((), jnp.int32)
    own_rank = jnp.sum(jnp.where(owned_rows, adapter_rank[None, :], zero_int), axis=1)
    own_slot = jnp.sum(jnp.where(owned_rows, adapter_slot[None, :], zero_int), axis=1)
    own_first = jnp.sum(jnp.where(owned_rows, begins[None, :], zero_int), axis=1)
    slot_hot = own_slot[:, None] == jnp.arange(TENANTS, dtype=jnp.int32)[None, :]
    return (own_rank, own_first, slot_hot)


def select_slot(down_values, slot_hot):
    shaped = down_values.reshape(down_values.shape[0], -1, TENANTS)
    return jnp.sum(jnp.where(slot_hot[:, None, :], shaped, 0.0), axis=2)


def scale_ranks(picked, own_rank, first_rank):
    rank_index = first_rank + jnp.arange(picked.shape[1], dtype=jnp.int32)
    keep_mask = rank_index[None, :] < own_rank[:, None]
    factor = ADAPTER_ALPHA / jnp.sqrt(own_rank.astype(jnp.float32))
    return jnp.where(keep_mask, picked * factor[:, None], 0.0).astype(jnp.bfloat16)


def widen_slots(low_values, slot_hot):
    wide_rows = jnp.where(
        slot_hot[:, None, :], low_values[:, :, None], jnp.zeros((), low_values.dtype)
    )
    return wide_rows.reshape(low_values.shape[0], -1)


def ring_reduce_scatter(blocks, axis):
    count = lax.axis_size(axis)
    me = lax.axis_index(axis)
    if count == 1:
        return blocks[0]
    shift = [(i, (i + 1) % count) for i in range(count)]

    def pick(step):
        return lax.dynamic_index_in_dim(blocks, (me - 1 - step) % count, 0, keepdims=False)

    total = pick(0)
    for step in range(1, count):
        total = lax.ppermute(total, axis, shift) + pick(step)
    return total


def shards(
    tokens,
    weight_query,
    weight_keyval,
    down_query,
    down_keyval,
    up_query,
    up_keyval,
    adapter_rank,
    token_lengths,
    adapter_slot,
):
    tensor_count = lax.axis_size("tensor")
    block_count = lax.axis_size(("seq", "load"))
    tensor_index = lax.axis_index("tensor")
    block_index = lax.axis_index(("seq", "load"))
    query_cols = weight_query.shape[1]
    keyval_cols = weight_keyval.shape[1]
    rank_share = down_query.shape[1] // TENANTS
    block_rows = tokens.shape[0] * tensor_count // block_count
    up_query_all = lax.all_gather(up_query, "load", axis=0, tiled=True)
    up_keyval_all = lax.all_gather(up_keyval, "load", axis=0, tiled=True)
    ring = tensor_count
    chunk = tokens.shape[0]
    small_cols = keyval_cols + 2 * rank_share
    small_terms = jnp.zeros((ring, chunk, small_cols), jnp.float32)
    query_terms = jnp.zeros((ring, chunk, query_cols), jnp.float32)
    shift = [(i, (i + 1) % ring) for i in range(ring)]
    held = tokens
    waiting = []
    for step in range(ring):
        following = lax.ppermute(held, "tensor", shift) if step < ring - 1 else None
        owner = (tensor_index - step) % ring
        if step == 1 and ring > 2:
            waiting.append((held, owner))
        else:
            batch = waiting + [(held, owner)] if step == ring - 1 else [(held, owner)]
            rows_now = jnp.concatenate([b for b, _ in batch], axis=0)
            block_ids = jnp.concatenate(
                [o * chunk + jnp.arange(chunk, dtype=jnp.int32) for _, o in batch]
            )
            _, _, block_hot = tenant_table(block_ids, adapter_rank, token_lengths, adapter_slot)
            small_rows = jnp.concatenate(
                [
                    product(rows_now, weight_keyval),
                    select_slot(product(rows_now, down_query), block_hot),
                    select_slot(product(rows_now, down_keyval), block_hot),
                ],
                axis=1,
            )
            for index, (_, o) in enumerate(batch):
                small_terms = lax.dynamic_update_slice_in_dim(
                    small_terms, small_rows[index * chunk : (index + 1) * chunk][None], o, 0
                )
        if step == 0 and ring > 2:
            first_block, first_owner = held, owner
        elif step == 1 and ring > 2:
            pair = product(jnp.concatenate([first_block, held], axis=0), weight_query)
            query_terms = lax.dynamic_update_slice_in_dim(
                query_terms, pair[:chunk][None], first_owner, 0
            )
            query_terms = lax.dynamic_update_slice_in_dim(
                query_terms, pair[chunk:][None], owner, 0
            )
        else:
            query_terms = lax.dynamic_update_slice_in_dim(
                query_terms, product(held, weight_query)[None], owner, 0
            )
        if following is not None:
            if step == 0 and ring > 2:
                following, small_terms, first_block = lax.optimization_barrier(
                    (following, small_terms, first_block)
                )
            else:
                following, small_terms, query_terms = lax.optimization_barrier(
                    (following, small_terms, query_terms)
                )
        held = following
    seq_count = lax.axis_size("seq")
    load_count = lax.axis_size("load")
    by_core = small_terms.reshape(seq_count, load_count, block_rows, -1)
    per_core = ring_reduce_scatter(jnp.moveaxis(by_core, 1, 0), "load")
    small_summed = ring_reduce_scatter(per_core, "seq")
    query_summed = lax.psum_scatter(
        query_terms.reshape(ring * chunk, -1), ("seq", "load"), scatter_dimension=0, tiled=True
    )
    token_ids = block_index * block_rows + jnp.arange(block_rows, dtype=jnp.int32)
    own_rank, own_first, slot_hot = tenant_table(
        token_ids, adapter_rank, token_lengths, adapter_slot
    )
    position = token_ids - own_first
    first_rank = tensor_index * rank_share
    low_query = scale_ranks(
        small_summed[:, keyval_cols : keyval_cols + rank_share], own_rank, first_rank
    )
    low_keyval = scale_ranks(small_summed[:, keyval_cols + rank_share :], own_rank, first_rank)
    low_both = lax.all_gather(
        jnp.concatenate([low_query, low_keyval], axis=1), "tensor", axis=1
    )
    full_query = low_both[:, :, :rank_share].reshape(block_rows, -1)
    full_keyval = low_both[:, :, rank_share:].reshape(block_rows, -1)
    wide_query = widen_slots(full_query, slot_hot)
    wide_keyval = widen_slots(full_keyval, slot_hot)
    delta_keyval = product(wide_keyval, up_keyval_all)
    keyval = small_summed[:, :keyval_cols] + delta_keyval
    kv_first_col = tensor_index * keyval_cols
    is_key = kv_first_col + jnp.arange(keyval_cols, dtype=jnp.int32) < KV_HEADS * HEAD_DIM
    kv_local = jnp.where(
        is_key[None, :], rotate_pairs(keyval, position, kv_first_col), keyval
    ).astype(jnp.bfloat16)
    kv_all = lax.all_gather(kv_local, "tensor", axis=1, tiled=True)
    heads_here = query_cols // HEAD_DIM
    group_size = HEADS // KV_HEADS
    kv_here = max(heads_here // group_size, 1)
    per_kv = heads_here // kv_here
    kv_first = tensor_index * heads_here // group_size
    key_cols = KV_HEADS * HEAD_DIM
    key_heads = lax.dynamic_slice_in_dim(
        kv_all, kv_first * HEAD_DIM, kv_here * HEAD_DIM, 1
    ).reshape(block_rows, kv_here, HEAD_DIM)
    value_heads = lax.dynamic_slice_in_dim(
        kv_all, key_cols + kv_first * HEAD_DIM, kv_here * HEAD_DIM, 1
    ).reshape(block_rows, kv_here, HEAD_DIM)
    both_heads = lax.all_gather(
        jnp.concatenate([key_heads, value_heads], axis=1), ("seq", "load"), axis=0, tiled=True
    )
    piece_keys = both_heads[:, :kv_here]
    piece_values = both_heads[:, kv_here:]
    delta_query = lax.optimization_barrier(product(wide_query, up_query_all))
    query_rows = rotate_pairs(
        query_summed + delta_query, position, tensor_index * query_cols
    ).astype(jnp.bfloat16)
    grouped = query_rows.reshape(block_rows, kv_here, per_kv, HEAD_DIM)
    key_ids = jnp.arange(piece_keys.shape[0], dtype=jnp.int32)
    visible = (key_ids[None, :] >= own_first[:, None]) & (key_ids[None, :] <= token_ids[:, None])
    scores = jnp.einsum(
        "qghd,kgd->ghqk", grouped, piece_keys, preferred_element_type=jnp.float32
    ) / math.sqrt(HEAD_DIM)
    scores = jnp.where(visible, scores, -1e30)
    row_top = jnp.max(scores, axis=3)
    exp_scores = jnp.where(visible, jnp.exp(scores - row_top[..., None]), 0.0)
    row_total = jnp.sum(exp_scores, axis=3)
    accumulated = jnp.einsum(
        "ghqk,kgd->ghqd",
        exp_scores.astype(jnp.bfloat16),
        piece_values,
        preferred_element_type=jnp.float32,
    )
    context = (accumulated / row_total[..., None]).astype(jnp.bfloat16)
    context = jnp.transpose(context, (2, 0, 1, 3)).reshape(block_rows, query_cols)
    return (context, kv_local)


def solution(mesh):
    placed = (
        P(("groups", "tensor"), ("seq", "load")),
        P(("seq", "load"), "tensor"),
        P(("seq", "load"), "tensor"),
        P(("seq", "load"), ("groups", "tensor")),
        P(("seq", "load"), ("groups", "tensor")),
        P(("groups", "load"), "tensor"),
        P(("groups", "load"), "tensor"),
        P("groups"),
        P("groups"),
        P("groups"),
    )
    return jax.shard_map(
        shards,
        mesh=mesh,
        in_specs=placed,
        out_specs=(P(("groups", "seq", "load"), "tensor"), P(("groups", "seq", "load"), "tensor")),
        check_vma=False,
    )
```
